1024 devices in a mesh: ctx: 64 (over z_lo, y, core), row: 4 (over x), col: 4 (over z_hi).
Axes of the slice: x: 4, y: 4, z: 32 (z_hi: 4, z_lo: 8; z = z_hi * 8 + z_lo), core: 2. Of those that a mesh axis runs over, the one named last changes fastest.
Arguments:
- tokens: bfloat16 [16384, 4096], P('ctx', 'col'), may hold values from -6 to 6
- w_xz: bfloat16 [4096, 80, 128], P('col', 'row'), may hold values from -0.09375 to 0.09375
- w_dt: bfloat16 [4096, 80], P('col', 'row'), may hold values from -0.1875 to 0.1875
- w_bc: bfloat16 [4096, 8, 256], P('col', 'row'), may hold values from -0.03125 to 0.03125
- conv_x: float32 [4, 80, 64], P(None, ('row', 'col')), may hold values from -3 to 3
- conv_x_bias: float32 [80, 64], P(('row', 'col')), may hold values from -1.5 to 1.5
- conv_bc: float32 [4, 8, 256], replicated, may hold values from -3 to 3
- conv_bc_bias: float32 [8, 256], replicated, may hold values from -1.5 to 1.5
- dt_bias: float32 [80], P(('row', 'col')), may hold values from -1 to 1
- a_log: float32 [80], P(('row', 'col')), as said below
- d_skip: float32 [80], P(('row', 'col')), may hold values from 0.5 to 1.5
- norm_gain: float32 [80, 64], P(('row', 'col')), may hold values from 0.5 to 1.5
- w_out: bfloat16 [80, 64, 4096], P(('row', 'col')), may hold values from -0.125 to 0.125
Outputs:
- mixed: float32 [16384, 4096], P('ctx', ('row', 'col'))
The draws below stay inside these ranges and needn't reach their ends.
Inputs may be any that keep to these rules, and one draw needn't show every extreme that they name: `a_log`: one logarithm of a decay rate a head.
All inputs are finite; a program needn't handle non-finite values.
Results may differ from the reference program's by a relative error of at most 0.04.
Values may be sent and summed in bfloat16 or wider, within the bound.
No kernel may reach another device: no remote copies, remote signals or barrier semaphores. Data moves between devices by JAX's collectives and lax.ppermute only.
A program may use at most 64 MiB of HBM per device.

```python
import math
import jax
import jax.numpy as jnp
from jax import lax

D = 4096
H = 80
P_SIZE = 64
N = 128
G = 8
K = 4
TOK_DEV = 256
TOKENS = 16384
N_CTX = 64
N_COL = 4


def draw_a_log(key, part):
    first, second, third, fourth = jax.random.split(key, 4)
    fast_share = 0.3
    middle_share = 0.4
    pick = jax.random.uniform(first, (H,), jnp.float32, 0.0, 1.0)
    slow_log = jax.random.uniform(second, (H,), jnp.float32, math.log(0.1), math.log(0.8)) - math.log(TOKENS)
    fast_log = jax.random.uniform(third, (H,), jnp.float32, math.log(0.02), math.log(0.06))
    middle_log = jax.random.uniform(fourth, (H,), jnp.float32, math.log(0.3), math.log(1.5)) - math.log(TOK_DEV)
    chosen = jnp.where(pick < fast_share, fast_log, jnp.where(pick < fast_share + middle_share, middle_log, slow_log))
    return chosen.astype(jnp.float32)


def spiked(values, own_key, source, target, blocks, factor):
    owner, partner = [(jnp.arange(values.shape[axis_at]) // (values.shape[axis_at] // blocks)).reshape([-1 if axis == axis_at else 1 for axis in range(values.ndim)]) for axis_at in (source, target)]
    chosen = jax.random.permutation(own_key, blocks)[partner]
    strong = (owner == chosen) | (owner == (partner + blocks // 2) % blocks)
    return jnp.where(strong, factor * values, values)


def steps_of(stream_key, dims, shards, least, top_value):
    gain, own = 1.0, jax.random.fold_in(stream_key, 6)
    for position, parts in shards:
        heights = jnp.exp(jax.random.uniform(jax.random.fold_in(own, position), (parts,), jnp.float32, least / len(shards), top_value / len(shards)))
        gain = gain * jnp.repeat(heights, dims[position] // parts).reshape([-1 if axis == position else 1 for axis in range(len(dims))])
    return gain


def centred(rng, dims, deviation, most, shards=(), held_as=jnp.bfloat16):
    result = jax.random.normal(rng, dims, jnp.float32) * deviation
    if len(shards) > 0:
        result = steps_of(rng, dims, shards, -0.22, 0.18) * result
    return jnp.clip(result, min=-most, max=most).astype(held_as)


def heavy_noise(rng, extent, spread, bound, shards, heavy, kind=jnp.bfloat16):
    values = spread * jax.random.normal(rng, extent, jnp.float32)
    if shards:
        values = values * steps_of(rng, extent, shards, -0.22, 0.18)
    return jnp.clip(spiked(values, jax.random.fold_in(rng, 3), *heavy), -bound, bound).astype(kind)


def setup_inputs(seed: int = 0) -> dict:
    key_of = jax.random.split(jax.random.key(seed), 14)
    return {
        "tokens": centred(key_of[0], (TOKENS, D), 1.0, 6.0, ((0, 64), (1, 4))),
        "w_xz": centred(key_of[1], (D, H, 2 * P_SIZE), D ** -0.5, 0.09375, ((0, 4), (1, 4))),
        "w_dt": centred(key_of[2], (D, H), (D // 4) ** -0.5, 0.1875, ((0, 4), (1, 4))),
        "w_bc": centred(key_of[3], (D, G, 2 * N), (D * 8) ** -0.5, 0.03125, ((0, 4), (1, 4))),
        "conv_x": centred(key_of[4], (K, H, P_SIZE), K ** -0.5, 3.0, ((1, 16),), jnp.float32),
        "conv_x_bias": centred(key_of[5], (H, P_SIZE), 0.3, 1.5, ((0, 16),), jnp.float32),
        "conv_bc": centred(key_of[6], (K, G, 2 * N), K ** -0.5, 3.0, (), jnp.float32),
        "conv_bc_bias": centred(key_of[7], (G, 2 * N), 0.3, 1.5, (), jnp.float32),
        "dt_bias": jnp.clip(jax.random.uniform(key_of[8], (H,), jnp.float32, -1.0, 1.0) * steps_of(key_of[8], (H,), ((0, 16),), -0.4, 0.0), -1.0, 1.0),
        "a_log": draw_a_log(jax.random.fold_in(key_of[13], 71), 0),
        "d_skip": jnp.clip(0.5 + 1.0 * jax.random.uniform(key_of[10], (H,), jnp.float32) ** steps_of(key_of[10], (H,), ((0, 16),), -0.2, 0.2), 0.5, 1.5),
        "norm_gain": jnp.clip(1.0 + 0.1 * jax.random.normal(key_of[11], (H, P_SIZE), jnp.float32), 0.5, 1.5),
        "w_out": heavy_noise(key_of[12], (H, P_SIZE, D), (H * P_SIZE) ** -0.5, 0.125, ((0, 16),), (0, 2, 16, 2.0)),
    }


EPSILON = 1e-05

def causal_conv(edge_rows, own_rows, weights, bias):
    width_k = weights.shape[0]
    count = own_rows.shape[0]
    joined = jnp.concatenate([edge_rows, own_rows], axis=0).astype(jnp.float32)
    total = bias.astype(jnp.float32) + jnp.zeros(own_rows.shape, jnp.float32)
    for offset in range(width_k):
        total = total + weights[offset] * joined[offset:offset + count]
    return jax.nn.silu(total).astype(jnp.bfloat16)

def reference(tokens, w_xz, w_dt, w_bc, conv_x, conv_x_bias, conv_bc, conv_bc_bias, dt_bias, a_log, d_skip, norm_gain, w_out):
    width = D // N_COL
    group_heads = H // G
    rate = jnp.exp(a_log)
    positions = jnp.arange(TOK_DEV)
    causal = positions[:, None] >= positions[None, :]
    out_matrix = w_out.reshape(H * P_SIZE, D)

    def block_step(carry, tok_block):
        x_edge, bc_edge, state_in = carry
        xz_sum = jnp.zeros((TOK_DEV, H, 2 * P_SIZE), jnp.float32)
        dt_raw = jnp.zeros((TOK_DEV, H), jnp.float32)
        bc_sum = jnp.zeros((TOK_DEV, G, 2 * N), jnp.float32)
        for column_block in range(N_COL):
            start = column_block * width
            piece = tok_block[:, start:start + width]
            xz_part = jnp.einsum('ld,dhe->lhe', piece.astype(jnp.float32), w_xz[start:start + width].astype(jnp.float32))
            dt_part = jnp.dot(piece, w_dt[start:start + width], preferred_element_type=jnp.float32)
            bc_part = jnp.einsum('ld,dgn->lgn', piece.astype(jnp.float32), w_bc[start:start + width].astype(jnp.float32))
            xz_sum = xz_sum + lax.optimization_barrier(xz_part.astype(jnp.bfloat16)).astype(jnp.float32)
            dt_raw = dt_raw + lax.optimization_barrier(dt_part.astype(jnp.bfloat16)).astype(jnp.float32)
            bc_sum = bc_sum + lax.optimization_barrier(bc_part.astype(jnp.bfloat16)).astype(jnp.float32)
        x_pre = xz_sum[:, :, :P_SIZE].astype(jnp.bfloat16)
        gate_z = xz_sum[:, :, P_SIZE:].astype(jnp.bfloat16)
        bc_pre = bc_sum.astype(jnp.bfloat16)
        x_conv = causal_conv(x_edge, x_pre, conv_x, conv_x_bias)
        bc_conv = causal_conv(bc_edge, bc_pre, conv_bc, conv_bc_bias)
        b_input = bc_conv[:, :, :N]
        c_output = bc_conv[:, :, N:]
        step_size = jax.nn.softplus(dt_raw + dt_bias)
        cumul = jnp.cumsum(step_size * rate, axis=0)
        cum_heads = cumul.T
        diff = cum_heads[:, :, None] - cum_heads[:, None, :]
        decay = jnp.where(causal[None], jnp.exp(-jnp.where(causal[None], diff, 0.0)), 0.0)
        scores = jnp.einsum('tgn,sgn->gts', c_output.astype(jnp.float32), b_input.astype(jnp.float32))
        scores_heads = jnp.repeat(scores, group_heads, axis=0)
        mixing = (scores_heads * decay * step_size.T[:, None, :]).astype(jnp.bfloat16)
        y_intra = jnp.einsum('hts,shp->thp', mixing.astype(jnp.float32), x_conv.astype(jnp.float32))
        b_heads = jnp.repeat(b_input, group_heads, axis=1)
        c_heads = jnp.repeat(c_output, group_heads, axis=1)
        tail = jnp.exp(-(cumul[-1][None, :] - cumul))
        scaled = ((tail * step_size)[:, :, None] * x_conv.astype(jnp.float32)).astype(jnp.bfloat16)
        local = jnp.einsum('shp,shn->hpn', scaled.astype(jnp.float32), b_heads.astype(jnp.float32))
        fall = jnp.exp(-cumul[-1])
        carried = jnp.einsum('thn,hpn->thp', c_heads.astype(jnp.float32), state_in, precision=lax.Precision.HIGHEST)
        y_total = y_intra + jnp.exp(-cumul)[:, :, None] * carried + d_skip[None, :, None] * x_conv.astype(jnp.float32)
        gated = y_total * jax.nn.silu(gate_z.astype(jnp.float32))
        grouped = gated.reshape(TOK_DEV, G, group_heads * P_SIZE)
        mean_sq = lax.optimization_barrier(jnp.sum(grouped * grouped, axis=2)) / (group_heads * P_SIZE)
        scale = jnp.repeat(lax.rsqrt(mean_sq + EPSILON), group_heads, axis=1)
        normed = (gated * scale[:, :, None] * norm_gain).astype(jnp.bfloat16)
        out_block = jnp.dot(normed.reshape(TOK_DEV, H * P_SIZE), out_matrix, preferred_element_type=jnp.float32)
        state_next = fall[:, None, None] * state_in + local
        return ((x_pre[TOK_DEV - K + 1:], bc_pre[TOK_DEV - K + 1:], state_next), out_block)
    init = (jnp.zeros((K - 1, H, P_SIZE), jnp.bfloat16), jnp.zeros((K - 1, G, 2 * N), jnp.bfloat16), jnp.zeros((H, P_SIZE, N), jnp.float32))
    final, outs = lax.scan(block_step, init, tokens.reshape(N_CTX, TOK_DEV, D))
    return outs.reshape(TOKENS, D)
```

```python
import jax
import jax.numpy as jnp
from jax import lax
from jax.sharding import PartitionSpec as P

EPSILON = 1e-05


def shifted(block, axis, distance):
    devices = range(lax.axis_size(axis))
    route = [(i - distance, i) for i in devices if i - distance in devices]
    return lax.ppermute(block, axis, route)


def causal_conv(edge_rows, own_rows, weights, bias):
    width_k = weights.shape[0]
    count = own_rows.shape[0]
    joined = jnp.concatenate([edge_rows, own_rows], axis=0).astype(jnp.float32)
    total = bias + jnp.zeros(own_rows.shape, jnp.float32)
    for offset in range(width_k):
        total = total + weights[offset] * joined[offset : offset + count]
    return jax.nn.silu(total).astype(jnp.bfloat16)


def combine_states(earlier, later):
    return (earlier[0] * later[0], later[0][:, None, None] * earlier[1] + later[1])


def entering(fall, local, axis):
    size, mine = lax.axis_size(axis), lax.axis_index(axis)
    rows = local.shape[1]
    packed = jnp.concatenate(
        [local, jnp.broadcast_to(fall[:, None, None], (local.shape[0], 1, local.shape[2]))], axis=1
    )
    got = shifted(packed, axis, 1)
    first = mine < 1
    identity = jnp.concatenate(
        [jnp.zeros_like(local), jnp.ones((local.shape[0], 1, local.shape[2]), local.dtype)], axis=1
    )
    acc = jnp.where(first, identity, got)
    distance = 1
    while distance < size:
        before = shifted(acc, axis, distance)
        later_fall = acc[:, rows:rows + 1, :]
        joined = jnp.concatenate(
            [later_fall * before[:, :rows] + acc[:, :rows], later_fall * before[:, rows:]], axis=1
        )
        acc = jnp.where(mine >= distance, joined, acc)
        distance *= 2
    return acc[:, rows, 0], acc[:, :rows]


def body(
    tokens,
    w_xz,
    w_dt,
    w_bc,
    conv_x,
    conv_x_bias,
    conv_bc,
    conv_bc_bias,
    dt_bias,
    a_log,
    d_skip,
    norm_gain,
    w_out,
):
    tok_rows = tokens.shape[0]
    row_count = lax.axis_size("row")
    col_count = lax.axis_size("col")
    heads_row = w_xz.shape[1]
    heads_dev = heads_row // col_count
    head_width = w_xz.shape[2] // 2
    groups_row = w_bc.shape[1]
    groups = groups_row * row_count
    state_width = w_bc.shape[2] // 2
    group_heads = heads_row * row_count // groups
    col_index = lax.axis_index("col")
    row_first = lax.axis_index("row") * col_count * heads_dev
    group_start = row_first // group_heads
    own_group = (row_first + col_index * heads_dev) // group_heads
    xz_term = jnp.einsum("ld,dhe->lhe", tokens, w_xz, preferred_element_type=jnp.float32)
    dt_term = jnp.dot(tokens, w_dt, preferred_element_type=jnp.float32)
    bc_part = jnp.einsum("ld,dgn->lgn", tokens, w_bc, preferred_element_type=jnp.float32)
    slot_group = (
        row_first + jnp.arange(col_count, dtype=jnp.int32) * heads_dev
    ) // group_heads - group_start
    bc_slots = jnp.zeros((tok_rows, col_count, 2 * state_width), jnp.float32)
    for member in range(groups_row):
        picked = (slot_group == member).astype(jnp.float32)
        bc_slots = bc_slots + bc_part[:, member][:, None, :] * picked[None, :, None]
    xz_slots = xz_term.reshape(tok_rows, col_count, heads_dev * 2 * head_width)
    main = jnp.concatenate([xz_slots, bc_slots], axis=2)
    feat = main.shape[2]
    dt_flat = dt_term.reshape(tok_rows, col_count, heads_dev).transpose(1, 2, 0).reshape(col_count, -1)
    dt_rows = -(-dt_flat.shape[1] // (8 * feat)) * 8
    dt_flat = jnp.pad(dt_flat, ((0, 0), (0, dt_rows * feat - dt_flat.shape[1])))
    dt_block = dt_flat.reshape(col_count, dt_rows, feat).transpose(1, 0, 2)
    packed = jnp.concatenate([main, dt_block], axis=0)
    summed = lax.optimization_barrier(
        lax.psum_scatter(packed.astype(jnp.bfloat16), "col", scatter_dimension=1, tiled=True)
    )[:, 0]
    xz_width = heads_dev * 2 * head_width
    xz_sum = summed[:tok_rows, :xz_width].reshape(tok_rows, heads_dev, 2 * head_width)
    bc_pre = summed[:tok_rows, xz_width:]
    dt_raw = (
        summed[tok_rows:].reshape(-1)[: heads_dev * tok_rows]
        .reshape(heads_dev, tok_rows)
        .T.astype(jnp.float32)
    )
    x_pre = xz_sum[:, :, :head_width]
    gate_z = xz_sum[:, :, head_width:]
    edge_len = conv_x.shape[0] - 1
    edge = jnp.concatenate(
        [x_pre[tok_rows - edge_len :].reshape(edge_len, -1), bc_pre[tok_rows - edge_len :]], axis=1
    )
    edge = shifted(edge, "ctx", 1)
    x_edge = edge[:, : heads_dev * head_width].reshape(edge_len, heads_dev, head_width)
    bc_edge = edge[:, heads_dev * head_width :]
    x_conv = causal_conv(x_edge, x_pre, conv_x, conv_x_bias)
    bc_kernel = lax.dynamic_index_in_dim(conv_bc, own_group, 1, keepdims=False)
    bc_offset = lax.dynamic_index_in_dim(conv_bc_bias, own_group, 0, keepdims=False)
    bc_conv = causal_conv(bc_edge, bc_pre, bc_kernel, bc_offset)
    b_input = bc_conv[:, :state_width]
    c_output = bc_conv[:, state_width:]
    step_size = jax.nn.softplus(dt_raw + dt_bias)
    cumul = jnp.cumsum(step_size * jnp.exp(a_log), axis=0)
    cum_heads = cumul.T
    diff = cum_heads[:, :, None] - cum_heads[:, None, :]
    positions = jnp.arange(tok_rows)
    causal = (positions[:, None] >= positions[None, :])[None]
    decay = jnp.where(causal, jnp.exp(-jnp.where(causal, diff, 0.0)), 0.0)
    scores = jnp.einsum("tn,sn->ts", c_output, b_input, preferred_element_type=jnp.float32)
    mixing = (scores[None] * decay * step_size.T[:, None, :]).astype(jnp.bfloat16)
    y_intra = jnp.einsum("hts,shp->thp", mixing, x_conv, preferred_element_type=jnp.float32)
    tail = jnp.exp(-(cumul[-1][None, :] - cumul))
    scaled = ((tail * step_size)[:, :, None] * x_conv.astype(jnp.float32)).astype(jnp.bfloat16)
    local = jnp.einsum("shp,sn->hpn", scaled, b_input, preferred_element_type=jnp.float32)
    fall = jnp.exp(-cumul[-1])
    _, state_in = entering(fall, local, "ctx")
    carried = jnp.einsum(
        "tn,hpn->thp", c_output.astype(jnp.float32), state_in, precision=lax.Precision.HIGHEST
    )
    y_total = (
        y_intra
        + jnp.exp(-cumul)[:, :, None] * carried
        + d_skip[None, :, None] * x_conv.astype(jnp.float32)
    )
    gated = y_total * jax.nn.silu(gate_z.astype(jnp.float32))
    squares = jnp.sum(gated * gated, axis=(1, 2))
    if group_heads == 2 * heads_dev:
        partner = [(c, c ^ 1) for c in range(col_count)]
        group_sum = squares + lax.ppermute(squares, "col", partner)
    else:
        selector = (jnp.arange(groups, dtype=jnp.int32) == own_group).astype(jnp.float32)
        group_sums = lax.psum(squares[:, None] * selector[None, :], ("row", "col"))
        group_sum = jnp.sum(group_sums * selector[None, :], axis=1)
    mean_sq = group_sum / (group_heads * head_width)
    normed = (gated * lax.rsqrt(mean_sq + EPSILON)[:, None, None] * norm_gain).astype(jnp.bfloat16)
    partial_out = jnp.einsum("lhp,hpd->ld", normed, w_out, preferred_element_type=jnp.float32)
    by_row = lax.psum_scatter(
        partial_out.astype(jnp.bfloat16), "row", scatter_dimension=1, tiled=True
    )
    mixed = lax.psum_scatter(by_row, "col", scatter_dimension=1, tiled=True)
    return mixed.astype(jnp.float32)


def solution(mesh):
    in_specs = (
        P("ctx", "col"),
        P("col", "row", None),
        P("col", "row"),
        P("col", "row", None),
        P(None, ("row", "col"), None),
        P(("row", "col"), None),
        P(),
        P(),
        P(("row", "col")),
        P(("row", "col")),
        P(("row", "col")),
        P(("row", "col"), None),
        P(("row", "col"), None, None),
    )
    out_specs = P("ctx", ("row", "col"))
    return jax.shard_map(body, mesh=mesh, in_specs=in_specs, out_specs=out_specs, check_vma=False)
```

```python
import jax
import jax.numpy as jnp
from jax import lax
from jax.sharding import PartitionSpec as P

EPSILON = 1e-05


def shifted(block, axis, distance):
    devices = range(lax.axis_size(axis))
    route = [(i - distance, i) for i in devices if i - distance in devices]
    return lax.ppermute(block, axis, route)


def causal_conv(edge_rows, own_rows, weights, bias):
    width_k = weights.shape[0]
    count = own_rows.shape[0]
    joined = jnp.concatenate([edge_rows, own_rows], axis=0).astype(jnp.float32)
    total = bias + jnp.zeros(own_rows.shape, jnp.float32)
    for offset in range(width_k):
        total = total + weights[offset] * joined[offset : offset + count]
    return jax.nn.silu(total).astype(jnp.bfloat16)


def combine_states(earlier, later):
    return (earlier[0] * later[0], later[0][:, None, None] * earlier[1] + later[1])


def entering(fall, local, axis, radix=4):
    size, mine = lax.axis_size(axis), lax.axis_index(axis)
    rows = local.shape[1]
    own = jnp.concatenate(
        [local, jnp.broadcast_to(fall[:, None, None], (local.shape[0], 1, local.shape[2]))], axis=1
    )
    identity = jnp.concatenate(
        [jnp.zeros_like(local), jnp.ones((local.shape[0], 1, local.shape[2]), local.dtype)], axis=1
    )

    def join(before, later):
        later_fall = later[:, rows : rows + 1, :]
        return jnp.concatenate(
            [later_fall * before[:, :rows] + later[:, :rows], later_fall * before[:, rows:]], axis=1
        )

    acc = identity
    for distance in range(radix, 0, -1):
        if distance < size:
            got = shifted(own, axis, distance)
            acc = jnp.where(mine >= distance, join(acc, got), acc)
    span = radix
    while span < size:
        parts = [(step * span, shifted(acc, axis, step * span)) for step in range(1, radix) if step * span < size]
        total = acc
        for distance, got in parts:
            total = jnp.where(mine >= distance, join(got, total), total)
        acc = total
        span *= radix
    return acc[:, rows, 0], acc[:, :rows]


def body(
    tokens,
    w_xz,
    w_dt,
    w_bc,
    conv_x,
    conv_x_bias,
    conv_bc,
    conv_bc_bias,
    dt_bias,
    a_log,
    d_skip,
    norm_gain,
    w_out,
):
    tok_rows = tokens.shape[0]
    row_count = lax.axis_size("row")
    col_count = lax.axis_size("col")
    heads_row = w_xz.shape[1]
    heads_dev = heads_row // col_count
    head_width = w_xz.shape[2] // 2
    groups_row = w_bc.shape[1]
    groups = groups_row * row_count
    state_width = w_bc.shape[2] // 2
    group_heads = heads_row * row_count // groups
    col_index = lax.axis_index("col")
    row_first = lax.axis_index("row") * col_count * heads_dev
    group_start = row_first // group_heads
    own_group = (row_first + col_index * heads_dev) // group_heads
    xz_term = jnp.dot(
        tokens, w_xz.reshape(w_xz.shape[0], -1), preferred_element_type=jnp.float32
    ).reshape(tok_rows, heads_row, w_xz.shape[2])
    dt_term = jnp.dot(tokens, w_dt, preferred_element_type=jnp.float32)
    bc_part = jnp.einsum("ld,dgn->lgn", tokens, w_bc, preferred_element_type=jnp.float32)
    slot_group = (
        row_first + jnp.arange(col_count, dtype=jnp.int32) * heads_dev
    ) // group_heads - group_start
    bc_slots = jnp.zeros((tok_rows, col_count, 2 * state_width), jnp.float32)
    for member in range(groups_row):
        picked = (slot_group == member).astype(jnp.float32)
        bc_slots = bc_slots + bc_part[:, member][:, None, :] * picked[None, :, None]
    xz_slots = xz_term.reshape(tok_rows, col_count, heads_dev * 2 * head_width)
    main = jnp.concatenate([xz_slots, bc_slots], axis=2)
    feat = main.shape[2]
    dt_flat = dt_term.reshape(tok_rows, col_count, heads_dev).transpose(1, 2, 0).reshape(col_count, -1)
    dt_rows = -(-dt_flat.shape[1] // (8 * feat)) * 8
    dt_flat = jnp.pad(dt_flat, ((0, 0), (0, dt_rows * feat - dt_flat.shape[1])))
    dt_block = dt_flat.reshape(col_count, dt_rows, feat).transpose(1, 0, 2)
    packed = jnp.concatenate([main, dt_block], axis=0)
    summed = lax.optimization_barrier(
        lax.psum_scatter(packed.astype(jnp.bfloat16), "col", scatter_dimension=1, tiled=True)
    )[:, 0]
    xz_width = heads_dev * 2 * head_width
    xz_sum = summed[:tok_rows, :xz_width].reshape(tok_rows, heads_dev, 2 * head_width)
    bc_pre = summed[:tok_rows, xz_width:]
    dt_raw = (
        summed[tok_rows:].reshape(-1)[: heads_dev * tok_rows]
        .reshape(heads_dev, tok_rows)
        .T.astype(jnp.float32)
    )
    x_pre = xz_sum[:, :, :head_width]
    gate_z = xz_sum[:, :, head_width:]
    edge_len = conv_x.shape[0] - 1
    edge = jnp.concatenate(
        [x_pre[tok_rows - edge_len :].reshape(edge_len, -1), bc_pre[tok_rows - edge_len :]], axis=1
    )
    edge = shifted(edge, "ctx", 1)
    x_edge = edge[:, : heads_dev * head_width].reshape(edge_len, heads_dev, head_width)
    bc_edge = edge[:, heads_dev * head_width :]
    x_conv = causal_conv(x_edge, x_pre, conv_x, conv_x_bias)
    bc_kernel = lax.dynamic_index_in_dim(conv_bc, own_group, 1, keepdims=False)
    bc_offset = lax.dynamic_index_in_dim(conv_bc_bias, own_group, 0, keepdims=False)
    bc_conv = causal_conv(bc_edge, bc_pre, bc_kernel, bc_offset)
    b_input = bc_conv[:, :state_width]
    c_output = bc_conv[:, state_width:]
    step_size = jax.nn.softplus(dt_raw + dt_bias)
    cumul = jnp.cumsum(step_size * jnp.exp(a_log), axis=0)
    cum_heads = cumul.T
    diff = cum_heads[:, :, None] - cum_heads[:, None, :]
    positions = jnp.arange(tok_rows)
    causal = (positions[:, None] >= positions[None, :])[None]
    decay = jnp.where(causal, jnp.exp(-jnp.where(causal, diff, 0.0)), 0.0)
    scores = jnp.einsum("tn,sn->ts", c_output, b_input, preferred_element_type=jnp.float32)
    mixing = (scores[None] * decay * step_size.T[:, None, :]).astype(jnp.bfloat16)
    y_intra = jnp.einsum("hts,shp->thp", mixing, x_conv, preferred_element_type=jnp.float32)
    tail = jnp.exp(-(cumul[-1][None, :] - cumul))
    scaled = ((tail * step_size)[:, :, None] * x_conv.astype(jnp.float32)).astype(jnp.bfloat16)
    local = jnp.einsum("shp,sn->hpn", scaled, b_input, preferred_element_type=jnp.float32)
    fall = jnp.exp(-cumul[-1])
    _, state_in = entering(fall, local, "ctx")
    carried = jnp.einsum(
        "tn,hpn->thp", c_output.astype(jnp.float32), state_in, precision=lax.Precision.HIGHEST
    )
    y_total = (
        y_intra
        + jnp.exp(-cumul)[:, :, None] * carried
        + d_skip[None, :, None] * x_conv.astype(jnp.float32)
    )
    gated = y_total * jax.nn.silu(gate_z.astype(jnp.float32))
    squares = jnp.sum(gated * gated, axis=(1, 2))
    if group_heads == 2 * heads_dev:
        partner = [(c, c ^ 1) for c in range(col_count)]
        group_sum = squares + lax.ppermute(squares, "col", partner)
    else:
        selector = (jnp.arange(groups, dtype=jnp.int32) == own_group).astype(jnp.float32)
        group_sums = lax.psum(squares[:, None] * selector[None, :], ("row", "col"))
        group_sum = jnp.sum(group_sums * selector[None, :], axis=1)
    mean_sq = group_sum / (group_heads * head_width)
    normed = (gated * lax.rsqrt(mean_sq + EPSILON)[:, None, None] * norm_gain).astype(jnp.bfloat16)
    partial_out = jnp.einsum("lhp,hpd->ld", normed, w_out, preferred_element_type=jnp.float32)
    mixed = lax.psum_scatter(
        partial_out.astype(jnp.bfloat16), ("row", "col"), scatter_dimension=1, tiled=True
    )
    return mixed.astype(jnp.float32)


def solution(mesh):
    in_specs = (
        P("ctx", "col"),
        P("col", "row", None),
        P("col", "row"),
        P("col", "row", None),
        P(None, ("row", "col"), None),
        P(("row", "col"), None),
        P(),
        P(),
        P(("row", "col")),
        P(("row", "col")),
        P(("row", "col")),
        P(("row", "col"), None),
        P(("row", "col"), None, None),
    )
    out_specs = P("ctx", ("row", "col"))
    return jax.shard_map(body, mesh=mesh, in_specs=in_specs, out_specs=out_specs, check_vma=False)
```

```python
import jax
import jax.numpy as jnp
from jax import lax
from jax.sharding import PartitionSpec as P

EPSILON = 1e-05


def shifted(block, axis, distance):
    devices = range(lax.axis_size(axis))
    route = [(i - distance, i) for i in devices if i - distance in devices]
    return lax.ppermute(block, axis, route)


def causal_conv(edge_rows, own_rows, weights, bias):
    width_k = weights.shape[0]
    count = own_rows.shape[0]
    joined = jnp.concatenate([edge_rows, own_rows], axis=0).astype(jnp.float32)
    total = bias + jnp.zeros(own_rows.shape, jnp.float32)
    for offset in range(width_k):
        total = total + weights[offset] * joined[offset : offset + count]
    return jax.nn.silu(total).astype(jnp.bfloat16)


def combine_states(earlier, later):
    return (earlier[0] * later[0], later[0][:, None, None] * earlier[1] + later[1])


def entering(fall, local, axis, radix=4):
    size, mine = lax.axis_size(axis), lax.axis_index(axis)
    rows = local.shape[1]
    own = jnp.concatenate(
        [local, jnp.broadcast_to(fall[:, None, None], (local.shape[0], 1, local.shape[2]))], axis=1
    )
    identity = jnp.concatenate(
        [jnp.zeros_like(local), jnp.ones((local.shape[0], 1, local.shape[2]), local.dtype)], axis=1
    )

    def join(before, later):
        later_fall = later[:, rows : rows + 1, :]
        return jnp.concatenate(
            [later_fall * before[:, :rows] + later[:, :rows], later_fall * before[:, rows:]], axis=1
        )

    acc = identity
    for distance in range(radix, 0, -1):
        if distance < size:
            got = shifted(own, axis, distance)
            acc = jnp.where(mine >= distance, join(acc, got), acc)
    span = radix
    while span < size:
        parts = [(step * span, shifted(acc, axis, step * span)) for step in range(1, radix) if step * span < size]
        total = acc
        for distance, got in parts:
            total = jnp.where(mine >= distance, join(got, total), total)
        acc = total
        span *= radix
    return acc[:, rows, 0], acc[:, :rows]


def body(
    tokens,
    w_xz,
    w_dt,
    w_bc,
    conv_x,
    conv_x_bias,
    conv_bc,
    conv_bc_bias,
    dt_bias,
    a_log,
    d_skip,
    norm_gain,
    w_out,
):
    tok_rows = tokens.shape[0]
    row_count = lax.axis_size("row")
    col_count = lax.axis_size("col")
    heads_row = w_xz.shape[1]
    heads_dev = heads_row // col_count
    head_width = w_xz.shape[2] // 2
    groups_row = w_bc.shape[1]
    groups = groups_row * row_count
    state_width = w_bc.shape[2] // 2
    group_heads = heads_row * row_count // groups
    col_index = lax.axis_index("col")
    row_first = lax.axis_index("row") * col_count * heads_dev
    group_start = row_first // group_heads
    own_group = (row_first + col_index * heads_dev) // group_heads
    xz_term = jnp.dot(
        tokens, w_xz.reshape(w_xz.shape[0], -1), preferred_element_type=jnp.float32
    ).reshape(tok_rows, heads_row, w_xz.shape[2])
    dt_term = jnp.dot(tokens, w_dt, preferred_element_type=jnp.float32)
    bc_part = jnp.einsum("ld,dgn->lgn", tokens, w_bc, preferred_element_type=jnp.float32)
    slot_group = (
        row_first + jnp.arange(col_count, dtype=jnp.int32) * heads_dev
    ) // group_heads - group_start
    paired = group_heads == 2 * heads_dev and col_count == 2 * groups_row
    if paired:
        bc_slots = bc_part.reshape(tok_rows, col_count, state_width)
    else:
        bc_slots = jnp.zeros((tok_rows, col_count, 2 * state_width), jnp.float32)
        for member in range(groups_row):
            picked = (slot_group == member).astype(jnp.float32)
            bc_slots = bc_slots + bc_part[:, member][:, None, :] * picked[None, :, None]
    xz_slots = xz_term.reshape(tok_rows, col_count, heads_dev * 2 * head_width)
    main = jnp.concatenate([xz_slots, bc_slots], axis=2)
    feat = main.shape[2]
    dt_flat = dt_term.reshape(tok_rows, col_count, heads_dev).transpose(1, 2, 0).reshape(col_count, -1)
    dt_rows = -(-dt_flat.shape[1] // (8 * feat)) * 8
    dt_flat = jnp.pad(dt_flat, ((0, 0), (0, dt_rows * feat - dt_flat.shape[1])))
    dt_block = dt_flat.reshape(col_count, dt_rows, feat).transpose(1, 0, 2)
    packed = jnp.concatenate([main, dt_block], axis=0)
    summed = lax.optimization_barrier(
        lax.psum_scatter(packed.astype(jnp.bfloat16), "col", scatter_dimension=1, tiled=True)
    )[:, 0]
    xz_width = heads_dev * 2 * head_width
    xz_sum = summed[:tok_rows, :xz_width].reshape(tok_rows, heads_dev, 2 * head_width)
    bc_pre = summed[:tok_rows, xz_width:]
    if paired:
        partner = [(c, c ^ 1) for c in range(col_count)]
        other = lax.ppermute(bc_pre, "col", partner)
        bc_pre = jnp.where(
            col_index % 2 == 0,
            jnp.concatenate([bc_pre, other], axis=1),
            jnp.concatenate([other, bc_pre], axis=1),
        )
    dt_raw = (
        summed[tok_rows:].reshape(-1)[: heads_dev * tok_rows]
        .reshape(heads_dev, tok_rows)
        .T.astype(jnp.float32)
    )
    x_pre = xz_sum[:, :, :head_width]
    gate_z = xz_sum[:, :, head_width:]
    edge_len = conv_x.shape[0] - 1
    edge = jnp.concatenate(
        [x_pre[tok_rows - edge_len :].reshape(edge_len, -1), bc_pre[tok_rows - edge_len :]], axis=1
    )
    edge = shifted(edge, "ctx", 1)
    x_edge = edge[:, : heads_dev * head_width].reshape(edge_len, heads_dev, head_width)
    bc_edge = edge[:, heads_dev * head_width :]
    x_conv = causal_conv(x_edge, x_pre, conv_x, conv_x_bias)
    bc_kernel = lax.dynamic_index_in_dim(conv_bc, own_group, 1, keepdims=False)
    bc_offset = lax.dynamic_index_in_dim(conv_bc_bias, own_group, 0, keepdims=False)
    bc_conv = causal_conv(bc_edge, bc_pre, bc_kernel, bc_offset)
    b_input = bc_conv[:, :state_width]
    c_output = bc_conv[:, state_width:]
    step_size = jax.nn.softplus(dt_raw + dt_bias)
    cumul = jnp.cumsum(step_size * jnp.exp(a_log), axis=0)
    cum_heads = cumul.T
    diff = cum_heads[:, :, None] - cum_heads[:, None, :]
    positions = jnp.arange(tok_rows)
    causal = (positions[:, None] >= positions[None, :])[None]
    decay = jnp.where(causal, jnp.exp(-jnp.where(causal, diff, 0.0)), 0.0)
    scores = jnp.einsum("tn,sn->ts", c_output, b_input, preferred_element_type=jnp.float32)
    mixing = (scores[None] * decay * step_size.T[:, None, :]).astype(jnp.bfloat16)
    y_intra = jnp.einsum("hts,shp->thp", mixing, x_conv, preferred_element_type=jnp.float32)
    tail = jnp.exp(-(cumul[-1][None, :] - cumul))
    scaled = ((tail * step_size)[:, :, None] * x_conv.astype(jnp.float32)).astype(jnp.bfloat16)
    local = jnp.einsum("shp,sn->hpn", scaled, b_input, preferred_element_type=jnp.float32)
    fall = jnp.exp(-cumul[-1])
    _, state_in = entering(fall, local, "ctx")
    carried = jnp.einsum(
        "tn,hpn->thp", c_output.astype(jnp.float32), state_in, precision=lax.Precision.HIGHEST
    )
    y_total = (
        y_intra
        + jnp.exp(-cumul)[:, :, None] * carried
        + d_skip[None, :, None] * x_conv.astype(jnp.float32)
    )
    gated = y_total * jax.nn.silu(gate_z.astype(jnp.float32))
    squares = jnp.sum(gated * gated, axis=(1, 2))
    if group_heads == 2 * heads_dev:
        partner = [(c, c ^ 1) for c in range(col_count)]
        group_sum = squares + lax.ppermute(squares, "col", partner)
    else:
        selector = (jnp.arange(groups, dtype=jnp.int32) == own_group).astype(jnp.float32)
        group_sums = lax.psum(squares[:, None] * selector[None, :], ("row", "col"))
        group_sum = jnp.sum(group_sums * selector[None, :], axis=1)
    mean_sq = group_sum / (group_heads * head_width)
    normed = (gated * lax.rsqrt(mean_sq + EPSILON)[:, None, None] * norm_gain).astype(jnp.bfloat16)
    partial_out = jnp.einsum("lhp,hpd->ld", normed, w_out, preferred_element_type=jnp.float32)
    by_row = lax.psum_scatter(
        partial_out.astype(jnp.bfloat16), "row", scatter_dimension=1, tiled=True
    )
    mixed = lax.psum_scatter(by_row, "col", scatter_dimension=1, tiled=True)
    return mixed.astype(jnp.float32)


def solution(mesh):
    in_specs = (
        P("ctx", "col"),
        P("col", "row", None),
        P("col", "row"),
        P("col", "row", None),
        P(None, ("row", "col"), None),
        P(("row", "col"), None),
        P(),
        P(),
        P(("row", "col")),
        P(("row", "col")),
        P(("row", "col")),
        P(("row", "col"), None),
        P(("row", "col"), None, None),
    )
    out_specs = P("ctx", ("row", "col"))
    return jax.shard_map(body, mesh=mesh, in_specs=in_specs, out_specs=out_specs, check_vma=False)
```

```python
import jax
import jax.numpy as jnp
from jax import lax
from jax.sharding import PartitionSpec as P

EPSILON = 1e-05


def shifted(block, axis, distance):
    devices = range(lax.axis_size(axis))
    route = [(i - distance, i) for i in devices if i - distance in devices]
    return lax.ppermute(block, axis, route)


def causal_conv(edge_rows, own_rows, weights, bias):
    width_k = weights.shape[0]
    count = own_rows.shape[0]
    joined = jnp.concatenate([edge_rows, own_rows], axis=0).astype(jnp.float32)
    total = bias + jnp.zeros(own_rows.shape, jnp.float32)
    for offset in range(width_k):
        total = total + weights[offset] * joined[offset : offset + count]
    return jax.nn.silu(total).astype(jnp.bfloat16)


def combine_states(earlier, later):
    return (earlier[0] * later[0], later[0][:, None, None] * earlier[1] + later[1])


def entering(fall, local, axis, radix=4):
    size, mine = lax.axis_size(axis), lax.axis_index(axis)
    rows = local.shape[1]
    own = jnp.concatenate(
        [local, jnp.broadcast_to(fall[:, None, None], (local.shape[0], 1, local.shape[2]))], axis=1
    )
    identity = jnp.concatenate(
        [jnp.zeros_like(local), jnp.ones((local.shape[0], 1, local.shape[2]), local.dtype)], axis=1
    )

    def join(before, later):
        later_fall = later[:, rows : rows + 1, :]
        return jnp.concatenate(
            [later_fall * before[:, :rows] + later[:, :rows], later_fall * before[:, rows:]], axis=1
        )

    acc = identity
    for distance in range(radix, 0, -1):
        if distance < size:
            got = shifted(own, axis, distance)
            acc = jnp.where(mine >= distance, join(acc, got), acc)
    span = radix
    while span < size:
        parts = [(step * span, shifted(acc, axis, step * span)) for step in range(1, radix) if step * span < size]
        total = acc
        for distance, got in parts:
            total = jnp.where(mine >= distance, join(got, total), total)
        acc = total
        span *= radix
    return acc[:, rows, 0], acc[:, :rows]


def body(
    tokens,
    w_xz,
    w_dt,
    w_bc,
    conv_x,
    conv_x_bias,
    conv_bc,
    conv_bc_bias,
    dt_bias,
    a_log,
    d_skip,
    norm_gain,
    w_out,
):
    tok_rows = tokens.shape[0]
    row_count = lax.axis_size("row")
    col_count = lax.axis_size("col")
    heads_row = w_xz.shape[1]
    heads_dev = heads_row // col_count
    head_width = w_xz.shape[2] // 2
    groups_row = w_bc.shape[1]
    groups = groups_row * row_count
    state_width = w_bc.shape[2] // 2
    group_heads = heads_row * row_count // groups
    col_index = lax.axis_index("col")
    row_first = lax.axis_index("row") * col_count * heads_dev
    group_start = row_first // group_heads
    own_group = (row_first + col_index * heads_dev) // group_heads
    xz_term = jnp.dot(
        tokens, w_xz.reshape(w_xz.shape[0], -1), preferred_element_type=jnp.float32
    ).reshape(tok_rows, heads_row, w_xz.shape[2])
    dt_term = jnp.dot(tokens, w_dt, preferred_element_type=jnp.float32)
    bc_part = jnp.einsum("ld,dgn->lgn", tokens, w_bc, preferred_element_type=jnp.float32)
    slot_group = (
        row_first + jnp.arange(col_count, dtype=jnp.int32) * heads_dev
    ) // group_heads - group_start
    bc_slots = jnp.zeros((tok_rows, col_count, 2 * state_width), jnp.float32)
    for member in range(groups_row):
        picked = (slot_group == member).astype(jnp.float32)
        bc_slots = bc_slots + bc_part[:, member][:, None, :] * picked[None, :, None]
    xz_slots = xz_term.reshape(tok_rows, col_count, heads_dev, 2 * head_width)
    x_width = heads_dev * head_width
    first = jnp.concatenate(
        [xz_slots[..., :head_width].reshape(tok_rows, col_count, x_width), bc_slots[..., :state_width]],
        axis=2,
    )
    feat = first.shape[2]
    dt_flat = dt_term.reshape(tok_rows, col_count, heads_dev).transpose(1, 2, 0).reshape(col_count, -1)
    dt_rows = -(-dt_flat.shape[1] // (8 * feat)) * 8
    dt_flat = jnp.pad(dt_flat, ((0, 0), (0, dt_rows * feat - dt_flat.shape[1])))
    dt_block = dt_flat.reshape(col_count, dt_rows, feat).transpose(1, 0, 2)
    first = jnp.concatenate([first, dt_block], axis=0)
    second = jnp.concatenate(
        [xz_slots[..., head_width:].reshape(tok_rows, col_count, x_width), bc_slots[..., state_width:]],
        axis=2,
    )
    summed = lax.optimization_barrier(
        lax.psum_scatter(first.astype(jnp.bfloat16), "col", scatter_dimension=1, tiled=True)
    )[:, 0]
    summed_late = lax.optimization_barrier(
        lax.psum_scatter(second.astype(jnp.bfloat16), "col", scatter_dimension=1, tiled=True)
    )[:, 0]
    x_pre = summed[:tok_rows, :x_width].reshape(tok_rows, heads_dev, head_width)
    b_pre = summed[:tok_rows, x_width:]
    dt_raw = (
        summed[tok_rows:].reshape(-1)[: heads_dev * tok_rows]
        .reshape(heads_dev, tok_rows)
        .T.astype(jnp.float32)
    )
    edge_len = conv_x.shape[0] - 1
    edge = jnp.concatenate(
        [x_pre[tok_rows - edge_len :].reshape(edge_len, -1), b_pre[tok_rows - edge_len :]], axis=1
    )
    edge = shifted(edge, "ctx", 1)
    x_edge = edge[:, :x_width].reshape(edge_len, heads_dev, head_width)
    b_edge = edge[:, x_width:]
    x_conv = causal_conv(x_edge, x_pre, conv_x, conv_x_bias)
    bc_kernel = lax.dynamic_index_in_dim(conv_bc, own_group, 1, keepdims=False)
    bc_offset = lax.dynamic_index_in_dim(conv_bc_bias, own_group, 0, keepdims=False)
    b_input = causal_conv(b_edge, b_pre, bc_kernel[:, :state_width], bc_offset[:state_width])
    step_size = jax.nn.softplus(dt_raw + dt_bias)
    cumul = jnp.cumsum(step_size * jnp.exp(a_log), axis=0)
    cum_heads = cumul.T
    diff = cum_heads[:, :, None] - cum_heads[:, None, :]
    positions = jnp.arange(tok_rows)
    causal = (positions[:, None] >= positions[None, :])[None]
    decay = jnp.where(causal, jnp.exp(-jnp.where(causal, diff, 0.0)), 0.0)
    tail = jnp.exp(-(cumul[-1][None, :] - cumul))
    scaled = ((tail * step_size)[:, :, None] * x_conv.astype(jnp.float32)).astype(jnp.bfloat16)
    local = jnp.einsum("shp,sn->hpn", scaled, b_input, preferred_element_type=jnp.float32)
    fall = jnp.exp(-cumul[-1])
    _, state_in = entering(fall, local, "ctx")
    state_in, summed_late = lax.optimization_barrier((state_in, summed_late))
    gate_z = summed_late[:, :x_width].reshape(tok_rows, heads_dev, head_width)
    c_pre = summed_late[:, x_width:]
    c_edge = shifted(c_pre[tok_rows - edge_len :], "ctx", 1)
    c_output = causal_conv(c_edge, c_pre, bc_kernel[:, state_width:], bc_offset[state_width:])
    scores = jnp.einsum("tn,sn->ts", c_output, b_input, preferred_element_type=jnp.float32)
    mixing = (scores[None] * decay * step_size.T[:, None, :]).astype(jnp.bfloat16)
    y_intra = jnp.einsum("hts,shp->thp", mixing, x_conv, preferred_element_type=jnp.float32)
    carried = jnp.einsum(
        "tn,hpn->thp", c_output.astype(jnp.float32), state_in, precision=lax.Precision.HIGHEST
    )
    y_total = (
        y_intra
        + jnp.exp(-cumul)[:, :, None] * carried
        + d_skip[None, :, None] * x_conv.astype(jnp.float32)
    )
    gated = y_total * jax.nn.silu(gate_z.astype(jnp.float32))
    squares = jnp.sum(gated * gated, axis=(1, 2))
    if group_heads == 2 * heads_dev:
        partner = [(c, c ^ 1) for c in range(col_count)]
        group_sum = squares + lax.ppermute(squares, "col", partner)
    else:
        selector = (jnp.arange(groups, dtype=jnp.int32) == own_group).astype(jnp.float32)
        group_sums = lax.psum(squares[:, None] * selector[None, :], ("row", "col"))
        group_sum = jnp.sum(group_sums * selector[None, :], axis=1)
    mean_sq = group_sum / (group_heads * head_width)
    normed = (gated * lax.rsqrt(mean_sq + EPSILON)[:, None, None] * norm_gain).astype(jnp.bfloat16)
    partial_out = jnp.einsum("lhp,hpd->ld", normed, w_out, preferred_element_type=jnp.float32)
    by_row = lax.psum_scatter(
        partial_out.astype(jnp.bfloat16), "row", scatter_dimension=1, tiled=True
    )
    mixed = lax.psum_scatter(by_row, "col", scatter_dimension=1, tiled=True)
    return mixed.astype(jnp.float32)


def solution(mesh):
    in_specs = (
        P("ctx", "col"),
        P("col", "row", None),
        P("col", "row"),
        P("col", "row", None),
        P(None, ("row", "col"), None),
        P(("row", "col"), None),
        P(),
        P(),
        P(("row", "col")),
        P(("row", "col")),
        P(("row", "col")),
        P(("row", "col"), None),
        P(("row", "col"), None, None),
    )
    out_specs = P("ctx", ("row", "col"))
    return jax.shard_map(body, mesh=mesh, in_specs=in_specs, out_specs=out_specs, check_vma=False)
```

```python
import jax
import jax.numpy as jnp
from jax import lax
from jax.sharding import PartitionSpec as P

EPSILON = 1e-05


def shifted(block, axis, distance):
    devices = range(lax.axis_size(axis))
    route = [(i - distance, i) for i in devices if i - distance in devices]
    return lax.ppermute(block, axis, route)


def shifted_narrow(block, axis, distance):
    return shifted(block.astype(jnp.bfloat16), axis, distance).astype(block.dtype)


def causal_conv(edge_rows, own_rows, weights, bias):
    width_k = weights.shape[0]
    count = own_rows.shape[0]
    joined = jnp.concatenate([edge_rows, own_rows], axis=0).astype(jnp.float32)
    total = bias + jnp.zeros(own_rows.shape, jnp.float32)
    for offset in range(width_k):
        total = total + weights[offset] * joined[offset : offset + count]
    return jax.nn.silu(total).astype(jnp.bfloat16)


def combine_states(earlier, later):
    return (earlier[0] * later[0], later[0][:, None, None] * earlier[1] + later[1])


def entering(fall, local, axis, radix=4):
    size, mine = lax.axis_size(axis), lax.axis_index(axis)
    rows = local.shape[1]
    own = jnp.concatenate(
        [local, jnp.broadcast_to(fall[:, None, None], (local.shape[0], 1, local.shape[2]))], axis=1
    )
    identity = jnp.concatenate(
        [jnp.zeros_like(local), jnp.ones((local.shape[0], 1, local.shape[2]), local.dtype)], axis=1
    )

    def join(before, later):
        later_fall = later[:, rows : rows + 1, :]
        return jnp.concatenate(
            [later_fall * before[:, :rows] + later[:, :rows], later_fall * before[:, rows:]], axis=1
        )

    acc = identity
    for distance in range(radix, 0, -1):
        if distance < size:
            got = shifted_narrow(own, axis, distance)
            acc = jnp.where(mine >= distance, join(acc, got), acc)
    span = radix
    while span < size:
        parts = [(step * span, shifted_narrow(acc, axis, step * span)) for step in range(1, radix) if step * span < size]
        total = acc
        for distance, got in parts:
            total = jnp.where(mine >= distance, join(got, total), total)
        acc = total
        span *= radix
    return acc[:, rows, 0], acc[:, :rows]


def body(
    tokens,
    w_xz,
    w_dt,
    w_bc,
    conv_x,
    conv_x_bias,
    conv_bc,
    conv_bc_bias,
    dt_bias,
    a_log,
    d_skip,
    norm_gain,
    w_out,
):
    tok_rows = tokens.shape[0]
    row_count = lax.axis_size("row")
    col_count = lax.axis_size("col")
    heads_row = w_xz.shape[1]
    heads_dev = heads_row // col_count
    head_width = w_xz.shape[2] // 2
    groups_row = w_bc.shape[1]
    groups = groups_row * row_count
    state_width = w_bc.shape[2] // 2
    group_heads = heads_row * row_count // groups
    col_index = lax.axis_index("col")
    row_first = lax.axis_index("row") * col_count * heads_dev
    group_start = row_first // group_heads
    own_group = (row_first + col_index * heads_dev) // group_heads
    xz_term = jnp.dot(
        tokens, w_xz.reshape(w_xz.shape[0], -1), preferred_element_type=jnp.float32
    ).reshape(tok_rows, heads_row, w_xz.shape[2])
    dt_term = jnp.dot(tokens, w_dt, preferred_element_type=jnp.float32)
    bc_part = jnp.einsum("ld,dgn->lgn", tokens, w_bc, preferred_element_type=jnp.float32)
    slot_group = (
        row_first + jnp.arange(col_count, dtype=jnp.int32) * heads_dev
    ) // group_heads - group_start
    paired = group_heads == 2 * heads_dev and col_count == 2 * groups_row
    if paired:
        bc_slots = bc_part.reshape(tok_rows, col_count, state_width)
    else:
        bc_slots = jnp.zeros((tok_rows, col_count, 2 * state_width), jnp.float32)
        for member in range(groups_row):
            picked = (slot_group == member).astype(jnp.float32)
            bc_slots = bc_slots + bc_part[:, member][:, None, :] * picked[None, :, None]
    xz_slots = xz_term.reshape(tok_rows, col_count, heads_dev * 2 * head_width)
    main = jnp.concatenate([xz_slots, bc_slots], axis=2)
    feat = main.shape[2]
    dt_flat = dt_term.reshape(tok_rows, col_count, heads_dev).transpose(1, 2, 0).reshape(col_count, -1)
    dt_rows = -(-dt_flat.shape[1] // (8 * feat)) * 8
    dt_flat = jnp.pad(dt_flat, ((0, 0), (0, dt_rows * feat - dt_flat.shape[1])))
    dt_block = dt_flat.reshape(col_count, dt_rows, feat).transpose(1, 0, 2)
    packed = jnp.concatenate([main, dt_block], axis=0)
    summed = lax.optimization_barrier(
        lax.psum_scatter(packed.astype(jnp.bfloat16), "col", scatter_dimension=1, tiled=True)
    )[:, 0]
    xz_width = heads_dev * 2 * head_width
    xz_sum = summed[:tok_rows, :xz_width].reshape(tok_rows, heads_dev, 2 * head_width)
    bc_pre = summed[:tok_rows, xz_width:]
    if paired:
        partner = [(c, c ^ 1) for c in range(col_count)]
        other = lax.ppermute(bc_pre, "col", partner)
        bc_pre = jnp.where(
            col_index % 2 == 0,
            jnp.concatenate([bc_pre, other], axis=1),
            jnp.concatenate([other, bc_pre], axis=1),
        )
    dt_raw = (
        summed[tok_rows:].reshape(-1)[: heads_dev * tok_rows]
        .reshape(heads_dev, tok_rows)
        .T.astype(jnp.float32)
    )
    x_pre = xz_sum[:, :, :head_width]
    gate_z = xz_sum[:, :, head_width:]
    edge_len = conv_x.shape[0] - 1
    edge = jnp.concatenate(
        [x_pre[tok_rows - edge_len :].reshape(edge_len, -1), bc_pre[tok_rows - edge_len :]], axis=1
    )
    edge = shifted(edge, "ctx", 1)
    x_edge = edge[:, : heads_dev * head_width].reshape(edge_len, heads_dev, head_width)
    bc_edge = edge[:, heads_dev * head_width :]
    x_conv = causal_conv(x_edge, x_pre, conv_x, conv_x_bias)
    bc_kernel = lax.dynamic_index_in_dim(conv_bc, own_group, 1, keepdims=False)
    bc_offset = lax.dynamic_index_in_dim(conv_bc_bias, own_group, 0, keepdims=False)
    bc_conv = causal_conv(bc_edge, bc_pre, bc_kernel, bc_offset)
    b_input = bc_conv[:, :state_width]
    c_output = bc_conv[:, state_width:]
    step_size = jax.nn.softplus(dt_raw + dt_bias)
    cumul = jnp.cumsum(step_size * jnp.exp(a_log), axis=0)
    cum_heads = cumul.T
    diff = cum_heads[:, :, None] - cum_heads[:, None, :]
    positions = jnp.arange(tok_rows)
    causal = (positions[:, None] >= positions[None, :])[None]
    decay = jnp.where(causal, jnp.exp(-jnp.where(causal, diff, 0.0)), 0.0)
    scores = jnp.einsum("tn,sn->ts", c_output, b_input, preferred_element_type=jnp.float32)
    mixing = (scores[None] * decay * step_size.T[:, None, :]).astype(jnp.bfloat16)
    y_intra = jnp.einsum("hts,shp->thp", mixing, x_conv, preferred_element_type=jnp.float32)
    tail = jnp.exp(-(cumul[-1][None, :] - cumul))
    scaled = ((tail * step_size)[:, :, None] * x_conv.astype(jnp.float32)).astype(jnp.bfloat16)
    local = jnp.einsum("shp,sn->hpn", scaled, b_input, preferred_element_type=jnp.float32)
    fall = jnp.exp(-cumul[-1])
    _, state_in = entering(fall, local, "ctx")
    carried = jnp.einsum(
        "tn,hpn->thp", c_output.astype(jnp.float32), state_in, precision=lax.Precision.HIGHEST
    )
    y_total = (
        y_intra
        + jnp.exp(-cumul)[:, :, None] * carried
        + d_skip[None, :, None] * x_conv.astype(jnp.float32)
    )
    gated = y_total * jax.nn.silu(gate_z.astype(jnp.float32))
    squares = jnp.sum(gated * gated, axis=(1, 2))
    if group_heads == 2 * heads_dev:
        partner = [(c, c ^ 1) for c in range(col_count)]
        group_sum = squares + lax.ppermute(squares, "col", partner)
    else:
        selector = (jnp.arange(groups, dtype=jnp.int32) == own_group).astype(jnp.float32)
        group_sums = lax.psum(squares[:, None] * selector[None, :], ("row", "col"))
        group_sum = jnp.sum(group_sums * selector[None, :], axis=1)
    mean_sq = group_sum / (group_heads * head_width)
    normed = (gated * lax.rsqrt(mean_sq + EPSILON)[:, None, None] * norm_gain).astype(jnp.bfloat16)
    partial_out = jnp.einsum("lhp,hpd->ld", normed, w_out, preferred_element_type=jnp.float32)
    row_index = lax.axis_index("row")
    shares = partial_out.astype(jnp.bfloat16).reshape(tok_rows, row_count, -1)
    by_row = lax.dynamic_index_in_dim(shares, row_index, 1, keepdims=False).astype(jnp.float32)
    for step in range(1, row_count):
        sent = lax.dynamic_index_in_dim(shares, (row_index + step) % row_count, 1, keepdims=False)
        route = [(j, (j + step) % row_count) for j in range(row_count)]
        by_row = by_row + lax.ppermute(sent, "row", route).astype(jnp.float32)
    by_row = by_row.astype(jnp.bfloat16)
    mixed = lax.psum_scatter(by_row, "col", scatter_dimension=1, tiled=True)
    return mixed.astype(jnp.float32)


def solution(mesh):
    in_specs = (
        P("ctx", "col"),
        P("col", "row", None),
        P("col", "row"),
        P("col", "row", None),
        P(None, ("row", "col"), None),
        P(("row", "col"), None),
        P(),
        P(),
        P(("row", "col")),
        P(("row", "col")),
        P(("row", "col")),
        P(("row", "col"), None),
        P(("row", "col"), None, None),
    )
    out_specs = P("ctx", ("row", "col"))
    return jax.shard_map(body, mesh=mesh, in_specs=in_specs, out_specs=out_specs, check_vma=False)
```

```python
import jax
import jax.numpy as jnp
from jax import lax
from jax.sharding import PartitionSpec as P

EPSILON = 1e-05


def shifted(block, axis, distance):
    devices = range(lax.axis_size(axis))
    route = [(i - distance, i) for i in devices if i - distance in devices]
    return lax.ppermute(block, axis, route)


def causal_conv(edge_rows, own_rows, weights, bias):
    width_k = weights.shape[0]
    count = own_rows.shape[0]
    joined = jnp.concatenate([edge_rows, own_rows], axis=0).astype(jnp.float32)
    total = bias + jnp.zeros(own_rows.shape, jnp.float32)
    for offset in range(width_k):
        total = total + weights[offset] * joined[offset : offset + count]
    return jax.nn.silu(total).astype(jnp.bfloat16)


def combine_states(earlier, later):
    return (earlier[0] * later[0], later[0][:, None, None] * earlier[1] + later[1])


def entering(fall, local, axis, radix=4):
    size, mine = lax.axis_size(axis), lax.axis_index(axis)
    rows = local.shape[1]
    own = jnp.concatenate(
        [local, jnp.broadcast_to(fall[:, None, None], (local.shape[0], 1, local.shape[2]))], axis=1
    )
    identity = jnp.concatenate(
        [jnp.zeros_like(local), jnp.ones((local.shape[0], 1, local.shape[2]), local.dtype)], axis=1
    )

    def join(before, later):
        later_fall = later[:, rows : rows + 1, :]
        return jnp.concatenate(
            [later_fall * before[:, :rows] + later[:, :rows], later_fall * before[:, rows:]], axis=1
        )

    acc = identity
    for distance in range(radix, 0, -1):
        if distance < size:
            got = shifted(own, axis, distance)
            acc = jnp.where(mine >= distance, join(acc, got), acc)
    span = radix
    while span < size:
        parts = [(step * span, shifted(acc, axis, step * span)) for step in range(1, radix) if step * span < size]
        total = acc
        for distance, got in parts:
            total = jnp.where(mine >= distance, join(got, total), total)
        acc = total
        span *= radix
    return acc[:, rows, 0], acc[:, :rows]


def body(
    tokens,
    w_xz,
    w_dt,
    w_bc,
    conv_x,
    conv_x_bias,
    conv_bc,
    conv_bc_bias,
    dt_bias,
    a_log,
    d_skip,
    norm_gain,
    w_out,
):
    tok_rows = tokens.shape[0]
    row_count = lax.axis_size("row")
    col_count = lax.axis_size("col")
    heads_row = w_xz.shape[1]
    heads_dev = heads_row // col_count
    head_width = w_xz.shape[2] // 2
    groups_row = w_bc.shape[1]
    groups = groups_row * row_count
    state_width = w_bc.shape[2] // 2
    group_heads = heads_row * row_count // groups
    col_index = lax.axis_index("col")
    row_first = lax.axis_index("row") * col_count * heads_dev
    group_start = row_first // group_heads
    own_group = (row_first + col_index * heads_dev) // group_heads
    xz_term = jnp.dot(
        tokens, w_xz.reshape(w_xz.shape[0], -1), preferred_element_type=jnp.float32
    ).reshape(tok_rows, heads_row, w_xz.shape[2])
    dt_term = jnp.dot(tokens, w_dt, preferred_element_type=jnp.float32)
    bc_part = jnp.einsum("ld,dgn->lgn", tokens, w_bc, preferred_element_type=jnp.float32)
    slot_group = (
        row_first + jnp.arange(col_count, dtype=jnp.int32) * heads_dev
    ) // group_heads - group_start
    paired = group_heads == 2 * heads_dev and col_count == 2 * groups_row
    if paired:
        bc_slots = bc_part.reshape(tok_rows, col_count, state_width)
    else:
        bc_slots = jnp.zeros((tok_rows, col_count, 2 * state_width), jnp.float32)
        for member in range(groups_row):
            picked = (slot_group == member).astype(jnp.float32)
            bc_slots = bc_slots + bc_part[:, member][:, None, :] * picked[None, :, None]
    xz_slots = xz_term.reshape(tok_rows, col_count, heads_dev * 2 * head_width)
    main = jnp.concatenate([xz_slots, bc_slots], axis=2)
    feat = main.shape[2]
    dt_flat = dt_term.reshape(tok_rows, col_count, heads_dev).transpose(1, 2, 0).reshape(col_count, -1)
    dt_rows = -(-dt_flat.shape[1] // (8 * feat)) * 8
    dt_flat = jnp.pad(dt_flat, ((0, 0), (0, dt_rows * feat - dt_flat.shape[1])))
    dt_block = dt_flat.reshape(col_count, dt_rows, feat).transpose(1, 0, 2)
    packed = jnp.concatenate([main, dt_block], axis=0)
    summed = lax.optimization_barrier(
        lax.psum_scatter(packed.astype(jnp.bfloat16), "col", scatter_dimension=1, tiled=True)
    )[:, 0]
    xz_width = heads_dev * 2 * head_width
    xz_sum = summed[:tok_rows, :xz_width].reshape(tok_rows, heads_dev, 2 * head_width)
    bc_pre = summed[:tok_rows, xz_width:]
    dt_raw = (
        summed[tok_rows:].reshape(-1)[: heads_dev * tok_rows]
        .reshape(heads_dev, tok_rows)
        .T.astype(jnp.float32)
    )
    x_pre = xz_sum[:, :, :head_width]
    gate_z = xz_sum[:, :, head_width:]
    edge_len = conv_x.shape[0] - 1
    edge = jnp.concatenate(
        [x_pre[tok_rows - edge_len :].reshape(edge_len, -1), bc_pre[tok_rows - edge_len :]], axis=1
    )
    edge = shifted(edge, "ctx", 1)
    x_edge = edge[:, : heads_dev * head_width].reshape(edge_len, heads_dev, head_width)
    bc_edge = edge[:, heads_dev * head_width :]
    if paired:
        partner = [(c, c ^ 1) for c in range(col_count)]
        other = lax.ppermute(bc_pre, "col", partner)
        ctx_count = lax.axis_size("ctx")
        diagonal = [
            ((i - 1) * col_count + (c ^ 1), i * col_count + c)
            for i in range(1, ctx_count)
            for c in range(col_count)
        ]
        other_edge = lax.ppermute(bc_pre[tok_rows - edge_len :], ("ctx", "col"), diagonal)
        low = col_index % 2 == 0
        bc_pre = jnp.where(
            low, jnp.concatenate([bc_pre, other], axis=1), jnp.concatenate([other, bc_pre], axis=1)
        )
        bc_edge = jnp.where(
            low,
            jnp.concatenate([bc_edge, other_edge], axis=1),
            jnp.concatenate([other_edge, bc_edge], axis=1),
        )
    x_conv = causal_conv(x_edge, x_pre, conv_x, conv_x_bias)
    bc_kernel = lax.dynamic_index_in_dim(conv_bc, own_group, 1, keepdims=False)
    bc_offset = lax.dynamic_index_in_dim(conv_bc_bias, own_group, 0, keepdims=False)
    bc_conv = causal_conv(bc_edge, bc_pre, bc_kernel, bc_offset)
    b_input = bc_conv[:, :state_width]
    c_output = bc_conv[:, state_width:]
    step_size = jax.nn.softplus(dt_raw + dt_bias)
    cumul = jnp.cumsum(step_size * jnp.exp(a_log), axis=0)
    cum_heads = cumul.T
    diff = cum_heads[:, :, None] - cum_heads[:, None, :]
    positions = jnp.arange(tok_rows)
    causal = (positions[:, None] >= positions[None, :])[None]
    decay = jnp.where(causal, jnp.exp(-jnp.where(causal, diff, 0.0)), 0.0)
    scores = jnp.einsum("tn,sn->ts", c_output, b_input, preferred_element_type=jnp.float32)
    mixing = (scores[None] * decay * step_size.T[:, None, :]).astype(jnp.bfloat16)
    y_intra = jnp.einsum("hts,shp->thp", mixing, x_conv, preferred_element_type=jnp.float32)
    tail = jnp.exp(-(cumul[-1][None, :] - cumul))
    scaled = ((tail * step_size)[:, :, None] * x_conv.astype(jnp.float32)).astype(jnp.bfloat16)
    local = jnp.einsum("shp,sn->hpn", scaled, b_input, preferred_element_type=jnp.float32)
    fall = jnp.exp(-cumul[-1])
    _, state_in = entering(fall, local, "ctx")
    carried = jnp.einsum(
        "tn,hpn->thp", c_output.astype(jnp.float32), state_in, precision=lax.Precision.HIGHEST
    )
    y_total = (
        y_intra
        + jnp.exp(-cumul)[:, :, None] * carried
        + d_skip[None, :, None] * x_conv.astype(jnp.float32)
    )
    gated = y_total * jax.nn.silu(gate_z.astype(jnp.float32))
    squares = jnp.sum(gated * gated, axis=(1, 2))
    if group_heads == 2 * heads_dev:
        partner = [(c, c ^ 1) for c in range(col_count)]
        group_sum = squares + lax.ppermute(squares, "col", partner)
    else:
        selector = (jnp.arange(groups, dtype=jnp.int32) == own_group).astype(jnp.float32)
        group_sums = lax.psum(squares[:, None] * selector[None, :], ("row", "col"))
        group_sum = jnp.sum(group_sums * selector[None, :], axis=1)
    mean_sq = group_sum / (group_heads * head_width)
    normed = (gated * lax.rsqrt(mean_sq + EPSILON)[:, None, None] * norm_gain).astype(jnp.bfloat16)
    partial_out = jnp.einsum("lhp,hpd->ld", normed, w_out, preferred_element_type=jnp.float32)
    swapped = lax.all_to_all(
        partial_out.astype(jnp.bfloat16), "row", split_axis=1, concat_axis=0, tiled=True
    )
    by_row = jnp.sum(
        swapped.reshape(row_count, tok_rows, -1).astype(jnp.float32), axis=0
    ).astype(jnp.bfloat16)
    mixed = lax.psum_scatter(by_row, "col", scatter_dimension=1, tiled=True)
    return mixed.astype(jnp.float32)


def solution(mesh):
    in_specs = (
        P("ctx", "col"),
        P("col", "row", None),
        P("col", "row"),
        P("col", "row", None),
        P(None, ("row", "col"), None),
        P(("row", "col"), None),
        P(),
        P(),
        P(("row", "col")),
        P(("row", "col")),
        P(("row", "col")),
        P(("row", "col"), None),
        P(("row", "col"), None, None),
    )
    out_specs = P("ctx", ("row", "col"))
    return jax.shard_map(body, mesh=mesh, in_specs=in_specs, out_specs=out_specs, check_vma=False)
```

```python
import jax
import jax.numpy as jnp
from jax import lax
from jax.sharding import PartitionSpec as P

EPSILON = 1e-05


def shifted(block, axis, distance):
    devices = range(lax.axis_size(axis))
    route = [(i - distance, i) for i in devices if i - distance in devices]
    return lax.ppermute(block, axis, route)


def shifted_narrow(block, axis, distance):
    return shifted(block.astype(jnp.bfloat16), axis, distance).astype(block.dtype)


def causal_conv(edge_rows, own_rows, weights, bias):
    width_k = weights.shape[0]
    count = own_rows.shape[0]
    joined = jnp.concatenate([edge_rows, own_rows], axis=0).astype(jnp.float32)
    total = bias + jnp.zeros(own_rows.shape, jnp.float32)
    for offset in range(width_k):
        total = total + weights[offset] * joined[offset : offset + count]
    return jax.nn.silu(total).astype(jnp.bfloat16)


def combine_states(earlier, later):
    return (earlier[0] * later[0], later[0][:, None, None] * earlier[1] + later[1])


def entering(fall, local, axis, radix=4):
    size, mine = lax.axis_size(axis), lax.axis_index(axis)
    rows = local.shape[1]
    own = jnp.concatenate(
        [local, jnp.broadcast_to(fall[:, None, None], (local.shape[0], 1, local.shape[2]))], axis=1
    )
    identity = jnp.concatenate(
        [jnp.zeros_like(local), jnp.ones((local.shape[0], 1, local.shape[2]), local.dtype)], axis=1
    )

    def join(before, later):
        later_fall = later[:, rows : rows + 1, :]
        return jnp.concatenate(
            [later_fall * before[:, :rows] + later[:, :rows], later_fall * before[:, rows:]], axis=1
        )

    acc = identity
    for distance in range(radix, 0, -1):
        if distance < size:
            got = shifted_narrow(own, axis, distance)
            acc = jnp.where(mine >= distance, join(acc, got), acc)
    span = radix
    while span < size:
        parts = [(step * span, shifted_narrow(acc, axis, step * span)) for step in range(1, radix) if step * span < size]
        total = acc
        for distance, got in parts:
            total = jnp.where(mine >= distance, join(got, total), total)
        acc = total
        span *= radix
    return acc[:, rows, 0], acc[:, :rows]


def body(
    tokens,
    w_xz,
    w_dt,
    w_bc,
    conv_x,
    conv_x_bias,
    conv_bc,
    conv_bc_bias,
    dt_bias,
    a_log,
    d_skip,
    norm_gain,
    w_out,
):
    tok_rows = tokens.shape[0]
    row_count = lax.axis_size("row")
    col_count = lax.axis_size("col")
    heads_row = w_xz.shape[1]
    heads_dev = heads_row // col_count
    head_width = w_xz.shape[2] // 2
    groups_row = w_bc.shape[1]
    groups = groups_row * row_count
    state_width = w_bc.shape[2] // 2
    group_heads = heads_row * row_count // groups
    col_index = lax.axis_index("col")
    row_first = lax.axis_index("row") * col_count * heads_dev
    group_start = row_first // group_heads
    own_group = (row_first + col_index * heads_dev) // group_heads
    xz_term = jnp.dot(
        tokens, w_xz.reshape(w_xz.shape[0], -1), preferred_element_type=jnp.float32
    ).reshape(tok_rows, heads_row, w_xz.shape[2])
    dt_term = jnp.dot(tokens, w_dt, preferred_element_type=jnp.float32)
    bc_part = jnp.einsum("ld,dgn->lgn", tokens, w_bc, preferred_element_type=jnp.float32)
    slot_group = (
        row_first + jnp.arange(col_count, dtype=jnp.int32) * heads_dev
    ) // group_heads - group_start
    paired = group_heads == 2 * heads_dev and col_count == 2 * groups_row
    if paired:
        bc_slots = bc_part.reshape(tok_rows, col_count, state_width)
    else:
        bc_slots = jnp.zeros((tok_rows, col_count, 2 * state_width), jnp.float32)
        for member in range(groups_row):
            picked = (slot_group == member).astype(jnp.float32)
            bc_slots = bc_slots + bc_part[:, member][:, None, :] * picked[None, :, None]
    xz_slots = xz_term.reshape(tok_rows, col_count, heads_dev * 2 * head_width)
    main = jnp.concatenate([xz_slots, bc_slots], axis=2)
    feat = main.shape[2]
    dt_flat = dt_term.reshape(tok_rows, col_count, heads_dev).transpose(1, 2, 0).reshape(col_count, -1)
    dt_rows = -(-dt_flat.shape[1] // (8 * feat)) * 8
    dt_flat = jnp.pad(dt_flat, ((0, 0), (0, dt_rows * feat - dt_flat.shape[1])))
    dt_block = dt_flat.reshape(col_count, dt_rows, feat).transpose(1, 0, 2)
    packed = jnp.concatenate([main, dt_block], axis=0)
    summed = lax.optimization_barrier(
        lax.psum_scatter(packed.astype(jnp.bfloat16), "col", scatter_dimension=1, tiled=True)
    )[:, 0]
    xz_width = heads_dev * 2 * head_width
    xz_sum = summed[:tok_rows, :xz_width].reshape(tok_rows, heads_dev, 2 * head_width)
    bc_pre = summed[:tok_rows, xz_width:]
    if paired:
        partner = [(c, c ^ 1) for c in range(col_count)]
        other = lax.ppermute(bc_pre, "col", partner)
        bc_pre = jnp.where(
            col_index % 2 == 0,
            jnp.concatenate([bc_pre, other], axis=1),
            jnp.concatenate([other, bc_pre], axis=1),
        )
    dt_raw = (
        summed[tok_rows:].reshape(-1)[: heads_dev * tok_rows]
        .reshape(heads_dev, tok_rows)
        .T.astype(jnp.float32)
    )
    x_pre = xz_sum[:, :, :head_width]
    gate_z = xz_sum[:, :, head_width:]
    edge_len = conv_x.shape[0] - 1
    edge = jnp.concatenate(
        [x_pre[tok_rows - edge_len :].reshape(edge_len, -1), bc_pre[tok_rows - edge_len :]], axis=1
    )
    edge = shifted(edge, "ctx", 1)
    x_edge = edge[:, : heads_dev * head_width].reshape(edge_len, heads_dev, head_width)
    bc_edge = edge[:, heads_dev * head_width :]
    x_conv = causal_conv(x_edge, x_pre, conv_x, conv_x_bias)
    bc_kernel = lax.dynamic_index_in_dim(conv_bc, own_group, 1, keepdims=False)
    bc_offset = lax.dynamic_index_in_dim(conv_bc_bias, own_group, 0, keepdims=False)
    bc_conv = causal_conv(bc_edge, bc_pre, bc_kernel, bc_offset)
    b_input = bc_conv[:, :state_width]
    c_output = bc_conv[:, state_width:]
    step_size = jax.nn.softplus(dt_raw + dt_bias)
    cumul = jnp.cumsum(step_size * jnp.exp(a_log), axis=0)
    cum_heads = cumul.T
    diff = cum_heads[:, :, None] - cum_heads[:, None, :]
    positions = jnp.arange(tok_rows)
    causal = (positions[:, None] >= positions[None, :])[None]
    decay = jnp.where(causal, jnp.exp(-jnp.where(causal, diff, 0.0)), 0.0)
    scores = jnp.einsum("tn,sn->ts", c_output, b_input, preferred_element_type=jnp.float32)
    mixing = (scores[None] * decay * step_size.T[:, None, :]).astype(jnp.bfloat16)
    y_intra = jnp.einsum("hts,shp->thp", mixing, x_conv, preferred_element_type=jnp.float32)
    tail = jnp.exp(-(cumul[-1][None, :] - cumul))
    scaled = ((tail * step_size)[:, :, None] * x_conv.astype(jnp.float32)).astype(jnp.bfloat16)
    local = jnp.einsum("shp,sn->hpn", scaled, b_input, preferred_element_type=jnp.float32)
    fall = jnp.exp(-cumul[-1])
    _, state_in = entering(fall, local, "ctx")
    carried = jnp.einsum(
        "tn,hpn->thp", c_output.astype(jnp.float32), state_in, precision=lax.Precision.HIGHEST
    )
    y_total = (
        y_intra
        + jnp.exp(-cumul)[:, :, None] * carried
        + d_skip[None, :, None] * x_conv.astype(jnp.float32)
    )
    gated = y_total * jax.nn.silu(gate_z.astype(jnp.float32))
    squares = jnp.sum(gated * gated, axis=(1, 2))
    if group_heads == 2 * heads_dev:
        partner = [(c, c ^ 1) for c in range(col_count)]
        group_sum = squares + lax.ppermute(squares, "col", partner)
    else:
        selector = (jnp.arange(groups, dtype=jnp.int32) == own_group).astype(jnp.float32)
        group_sums = lax.psum(squares[:, None] * selector[None, :], ("row", "col"))
        group_sum = jnp.sum(group_sums * selector[None, :], axis=1)
    mean_sq = group_sum / (group_heads * head_width)
    normed = (gated * lax.rsqrt(mean_sq + EPSILON)[:, None, None] * norm_gain).astype(jnp.bfloat16)
    partial_out = jnp.einsum("lhp,hpd->ld", normed, w_out, preferred_element_type=jnp.float32)
    swapped = lax.all_to_all(
        partial_out.astype(jnp.bfloat16), "row", split_axis=1, concat_axis=0, tiled=True
    )
    by_row = jnp.sum(
        swapped.reshape(row_count, tok_rows, -1).astype(jnp.float32), axis=0
    ).astype(jnp.bfloat16)
    mixed = lax.psum_scatter(by_row, "col", scatter_dimension=1, tiled=True)
    return mixed.astype(jnp.float32)


def solution(mesh):
    in_specs = (
        P("ctx", "col"),
        P("col", "row", None),
        P("col", "row"),
        P("col", "row", None),
        P(None, ("row", "col"), None),
        P(("row", "col"), None),
        P(),
        P(),
        P(("row", "col")),
        P(("row", "col")),
        P(("row", "col")),
        P(("row", "col"), None),
        P(("row", "col"), None, None),
    )
    out_specs = P("ctx", ("row", "col"))
    return jax.shard_map(body, mesh=mesh, in_specs=in_specs, out_specs=out_specs, check_vma=False)
```

```python
import jax
import jax.numpy as jnp
from jax import lax
from jax.sharding import PartitionSpec as P

EPSILON = 1e-05


def shifted(block, axis, distance):
    devices = range(lax.axis_size(axis))
    route = [(i - distance, i) for i in devices if i - distance in devices]
    return lax.ppermute(block, axis, route)


def shifted_narrow(block, axis, distance):
    return shifted(block.astype(jnp.bfloat16), axis, distance).astype(block.dtype)


def causal_conv(edge_rows, own_rows, weights, bias):
    width_k = weights.shape[0]
    count = own_rows.shape[0]
    joined = jnp.concatenate([edge_rows, own_rows], axis=0).astype(jnp.float32)
    total = bias + jnp.zeros(own_rows.shape, jnp.float32)
    for offset in range(width_k):
        total = total + weights[offset] * joined[offset : offset + count]
    return jax.nn.silu(total).astype(jnp.bfloat16)


def combine_states(earlier, later):
    return (earlier[0] * later[0], later[0][:, None, None] * earlier[1] + later[1])


def entering(fall, local, axis, radix=4):
    size, mine = lax.axis_size(axis), lax.axis_index(axis)
    rows = local.shape[1]
    own = jnp.concatenate(
        [local, jnp.broadcast_to(fall[:, None, None], (local.shape[0], 1, local.shape[2]))], axis=1
    )
    identity = jnp.concatenate(
        [jnp.zeros_like(local), jnp.ones((local.shape[0], 1, local.shape[2]), local.dtype)], axis=1
    )

    def join(before, later):
        later_fall = later[:, rows : rows + 1, :]
        return jnp.concatenate(
            [later_fall * before[:, :rows] + later[:, :rows], later_fall * before[:, rows:]], axis=1
        )

    acc = identity
    for distance in range(radix, 0, -1):
        if distance < size:
            got = shifted_narrow(own, axis, distance)
            acc = jnp.where(mine >= distance, join(acc, got), acc)
    span = radix
    while span < size:
        parts = [(step * span, shifted_narrow(acc, axis, step * span)) for step in range(1, radix) if step * span < size]
        total = acc
        for distance, got in parts:
            total = jnp.where(mine >= distance, join(got, total), total)
        acc = total
        span *= radix
    return acc[:, rows, 0], acc[:, :rows]


def body(
    tokens,
    w_xz,
    w_dt,
    w_bc,
    conv_x,
    conv_x_bias,
    conv_bc,
    conv_bc_bias,
    dt_bias,
    a_log,
    d_skip,
    norm_gain,
    w_out,
):
    tok_rows = tokens.shape[0]
    row_count = lax.axis_size("row")
    col_count = lax.axis_size("col")
    heads_row = w_xz.shape[1]
    heads_dev = heads_row // col_count
    head_width = w_xz.shape[2] // 2
    groups_row = w_bc.shape[1]
    groups = groups_row * row_count
    state_width = w_bc.shape[2] // 2
    group_heads = heads_row * row_count // groups
    col_index = lax.axis_index("col")
    row_first = lax.axis_index("row") * col_count * heads_dev
    group_start = row_first // group_heads
    own_group = (row_first + col_index * heads_dev) // group_heads
    xz_term = jnp.dot(
        tokens, w_xz.reshape(w_xz.shape[0], -1), preferred_element_type=jnp.float32
    ).reshape(tok_rows, heads_row, w_xz.shape[2])
    dt_term = jnp.dot(tokens, w_dt, preferred_element_type=jnp.float32)
    bc_part = jnp.einsum("ld,dgn->lgn", tokens, w_bc, preferred_element_type=jnp.float32)
    slot_group = (
        row_first + jnp.arange(col_count, dtype=jnp.int32) * heads_dev
    ) // group_heads - group_start
    paired = group_heads == 2 * heads_dev and col_count == 2 * groups_row
    if paired:
        bc_slots = bc_part.reshape(tok_rows, col_count, state_width)
    else:
        bc_slots = jnp.zeros((tok_rows, col_count, 2 * state_width), jnp.float32)
        for member in range(groups_row):
            picked = (slot_group == member).astype(jnp.float32)
            bc_slots = bc_slots + bc_part[:, member][:, None, :] * picked[None, :, None]
    xz_slots = xz_term.reshape(tok_rows, col_count, heads_dev * 2 * head_width)
    main = jnp.concatenate([xz_slots, bc_slots], axis=2)
    feat = main.shape[2]
    dt_flat = dt_term.reshape(tok_rows, col_count, heads_dev).transpose(1, 2, 0).reshape(col_count, -1)
    dt_rows = -(-dt_flat.shape[1] // (8 * feat)) * 8
    dt_flat = jnp.pad(dt_flat, ((0, 0), (0, dt_rows * feat - dt_flat.shape[1])))
    dt_block = dt_flat.reshape(col_count, dt_rows, feat).transpose(1, 0, 2)
    packed = jnp.concatenate([main, dt_block], axis=0)
    summed = lax.optimization_barrier(
        lax.psum_scatter(packed.astype(jnp.bfloat16), "col", scatter_dimension=1, tiled=True)
    )[:, 0]
    xz_width = heads_dev * 2 * head_width
    xz_sum = summed[:tok_rows, :xz_width].reshape(tok_rows, heads_dev, 2 * head_width)
    bc_pre = summed[:tok_rows, xz_width:]
    if paired:
        partner = [(c, c ^ 1) for c in range(col_count)]
        other = lax.ppermute(bc_pre, "col", partner)
        bc_pre = jnp.where(
            col_index % 2 == 0,
            jnp.concatenate([bc_pre, other], axis=1),
            jnp.concatenate([other, bc_pre], axis=1),
        )
    dt_raw = (
        summed[tok_rows:].reshape(-1)[: heads_dev * tok_rows]
        .reshape(heads_dev, tok_rows)
        .T.astype(jnp.float32)
    )
    x_pre = xz_sum[:, :, :head_width]
    gate_z = xz_sum[:, :, head_width:]
    edge_len = conv_x.shape[0] - 1
    edge = jnp.concatenate(
        [x_pre[tok_rows - edge_len :].reshape(edge_len, -1), bc_pre[tok_rows - edge_len :]], axis=1
    )
    edge = shifted(edge, "ctx", 1)
    x_edge = edge[:, : heads_dev * head_width].reshape(edge_len, heads_dev, head_width)
    bc_edge = edge[:, heads_dev * head_width :]
    x_conv = causal_conv(x_edge, x_pre, conv_x, conv_x_bias)
    bc_kernel = lax.dynamic_index_in_dim(conv_bc, own_group, 1, keepdims=False)
    bc_offset = lax.dynamic_index_in_dim(conv_bc_bias, own_group, 0, keepdims=False)
    bc_conv = causal_conv(bc_edge, bc_pre, bc_kernel, bc_offset)
    b_input = bc_conv[:, :state_width]
    c_output = bc_conv[:, state_width:]
    step_size = jax.nn.softplus(dt_raw + dt_bias)
    cumul = jnp.cumsum(step_size * jnp.exp(a_log), axis=0)
    cum_heads = cumul.T
    diff = cum_heads[:, :, None] - cum_heads[:, None, :]
    positions = jnp.arange(tok_rows)
    causal = (positions[:, None] >= positions[None, :])[None]
    decay = jnp.where(causal, jnp.exp(-jnp.where(causal, diff, 0.0)), 0.0)
    scores = jnp.einsum("tn,sn->ts", c_output, b_input, preferred_element_type=jnp.float32)
    mixing = (scores[None] * decay * step_size.T[:, None, :]).astype(jnp.bfloat16)
    y_intra = jnp.einsum("hts,shp->thp", mixing, x_conv, preferred_element_type=jnp.float32)
    tail = jnp.exp(-(cumul[-1][None, :] - cumul))
    scaled = ((tail * step_size)[:, :, None] * x_conv.astype(jnp.float32)).astype(jnp.bfloat16)
    local = jnp.einsum("shp,sn->hpn", scaled, b_input, preferred_element_type=jnp.float32)
    fall = jnp.exp(-cumul[-1])
    _, state_in = entering(fall, local, "ctx")
    carried = jnp.einsum(
        "tn,hpn->thp", c_output.astype(jnp.float32), state_in, precision=lax.Precision.HIGHEST
    )
    y_total = (
        y_intra
        + jnp.exp(-cumul)[:, :, None] * carried
        + d_skip[None, :, None] * x_conv.astype(jnp.float32)
    )
    gated = y_total * jax.nn.silu(gate_z.astype(jnp.float32))
    squares = jnp.sum(gated * gated, axis=(1, 2))
    if group_heads == 2 * heads_dev:
        partner = [(c, c ^ 1) for c in range(col_count)]
        group_sum = squares + lax.ppermute(squares, "col", partner)
    else:
        selector = (jnp.arange(groups, dtype=jnp.int32) == own_group).astype(jnp.float32)
        group_sums = lax.psum(squares[:, None] * selector[None, :], ("row", "col"))
        group_sum = jnp.sum(group_sums * selector[None, :], axis=1)
    mean_sq = group_sum / (group_heads * head_width)
    normed = (gated * lax.rsqrt(mean_sq + EPSILON)[:, None, None] * norm_gain).astype(jnp.bfloat16)
    partial_out = jnp.einsum("lhp,hpd->ld", normed, w_out, preferred_element_type=jnp.float32)
    swapped = lax.all_to_all(
        partial_out.astype(jnp.bfloat16), "row", split_axis=1, concat_axis=0, tiled=True
    )
    by_row = jnp.sum(
        swapped.reshape(row_count, tok_rows, -1).astype(jnp.float32), axis=0
    ).astype(jnp.bfloat16)
    crossed = lax.all_to_all(by_row, "col", split_axis=1, concat_axis=0, tiled=True)
    return jnp.sum(crossed.reshape(col_count, tok_rows, -1).astype(jnp.float32), axis=0)


def solution(mesh):
    in_specs = (
        P("ctx", "col"),
        P("col", "row", None),
        P("col", "row"),
        P("col", "row", None),
        P(None, ("row", "col"), None),
        P(("row", "col"), None),
        P(),
        P(),
        P(("row", "col")),
        P(("row", "col")),
        P(("row", "col")),
        P(("row", "col"), None),
        P(("row", "col"), None, None),
    )
    out_specs = P("ctx", ("row", "col"))
    return jax.shard_map(body, mesh=mesh, in_specs=in_specs, out_specs=out_specs, check_vma=False)
```

```python
import jax
import jax.numpy as jnp
from jax import lax
from jax.sharding import PartitionSpec as P

EPSILON = 1e-05


def shifted(block, axis, distance):
    devices = range(lax.axis_size(axis))
    route = [(i - distance, i) for i in devices if i - distance in devices]
    return lax.ppermute(block, axis, route)


def shifted_narrow(block, axis, distance):
    return shifted(block.astype(jnp.bfloat16), axis, distance).astype(block.dtype)


def causal_conv(edge_rows, own_rows, weights, bias):
    width_k = weights.shape[0]
    count = own_rows.shape[0]
    joined = jnp.concatenate([edge_rows, own_rows], axis=0).astype(jnp.float32)
    total = bias + jnp.zeros(own_rows.shape, jnp.float32)
    for offset in range(width_k):
        total = total + weights[offset] * joined[offset : offset + count]
    return jax.nn.silu(total).astype(jnp.bfloat16)


def combine_states(earlier, later):
    return (earlier[0] * later[0], later[0][:, None, None] * earlier[1] + later[1])


def entering(fall, local, axis, radix=4):
    size, mine = lax.axis_size(axis), lax.axis_index(axis)
    rows = local.shape[1]
    own = jnp.concatenate(
        [local, jnp.broadcast_to(fall[:, None, None], (local.shape[0], 1, local.shape[2]))], axis=1
    )
    identity = jnp.concatenate(
        [jnp.zeros_like(local), jnp.ones((local.shape[0], 1, local.shape[2]), local.dtype)], axis=1
    )

    def join(before, later):
        later_fall = later[:, rows : rows + 1, :]
        return jnp.concatenate(
            [later_fall * before[:, :rows] + later[:, :rows], later_fall * before[:, rows:]], axis=1
        )

    acc = identity
    for distance in range(radix, 0, -1):
        if distance < size:
            got = shifted_narrow(own, axis, distance)
            acc = jnp.where(mine >= distance, join(acc, got), acc)
    span = radix
    while span < size:
        parts = [(step * span, shifted_narrow(acc, axis, step * span)) for step in range(1, radix) if step * span < size]
        total = acc
        for distance, got in parts:
            total = jnp.where(mine >= distance, join(got, total), total)
        acc = total
        span *= radix
    return acc[:, rows, 0], acc[:, :rows]


def body(
    tokens,
    w_xz,
    w_dt,
    w_bc,
    conv_x,
    conv_x_bias,
    conv_bc,
    conv_bc_bias,
    dt_bias,
    a_log,
    d_skip,
    norm_gain,
    w_out,
):
    tok_rows = tokens.shape[0]
    row_count = lax.axis_size("row")
    col_count = lax.axis_size("col")
    heads_row = w_xz.shape[1]
    heads_dev = heads_row // col_count
    head_width = w_xz.shape[2] // 2
    groups_row = w_bc.shape[1]
    groups = groups_row * row_count
    state_width = w_bc.shape[2] // 2
    group_heads = heads_row * row_count // groups
    col_index = lax.axis_index("col")
    row_first = lax.axis_index("row") * col_count * heads_dev
    group_start = row_first // group_heads
    own_group = (row_first + col_index * heads_dev) // group_heads
    xz_term = jnp.dot(
        tokens, w_xz.reshape(w_xz.shape[0], -1), preferred_element_type=jnp.float32
    ).reshape(tok_rows, heads_row, w_xz.shape[2])
    dt_term = jnp.dot(tokens, w_dt, preferred_element_type=jnp.float32)
    bc_part = jnp.einsum("ld,dgn->lgn", tokens, w_bc, preferred_element_type=jnp.float32)
    slot_group = (
        row_first + jnp.arange(col_count, dtype=jnp.int32) * heads_dev
    ) // group_heads - group_start
    paired = group_heads == 2 * heads_dev and col_count == 2 * groups_row
    if paired:
        bc_slots = bc_part.reshape(tok_rows, col_count, state_width)
    else:
        bc_slots = jnp.zeros((tok_rows, col_count, 2 * state_width), jnp.float32)
        for member in range(groups_row):
            picked = (slot_group == member).astype(jnp.float32)
            bc_slots = bc_slots + bc_part[:, member][:, None, :] * picked[None, :, None]
    xz_slots = xz_term.reshape(tok_rows, col_count, heads_dev * 2 * head_width)
    main = jnp.concatenate([xz_slots, bc_slots], axis=2)
    feat = main.shape[2]
    dt_flat = dt_term.reshape(tok_rows, col_count, heads_dev).transpose(1, 2, 0).reshape(col_count, -1)
    dt_rows = -(-dt_flat.shape[1] // (8 * feat)) * 8
    dt_flat = jnp.pad(dt_flat, ((0, 0), (0, dt_rows * feat - dt_flat.shape[1])))
    dt_block = dt_flat.reshape(col_count, dt_rows, feat).transpose(1, 0, 2)
    packed = jnp.concatenate([main, dt_block], axis=0)
    crossed = lax.all_to_all(
        packed.astype(jnp.bfloat16), "col", split_axis=1, concat_axis=1, tiled=True
    )
    summed_wide = jnp.sum(crossed.astype(jnp.float32), axis=1)
    summed = summed_wide.astype(jnp.bfloat16)
    xz_width = heads_dev * 2 * head_width
    xz_sum = summed[:tok_rows, :xz_width].reshape(tok_rows, heads_dev, 2 * head_width)
    bc_pre = summed[:tok_rows, xz_width:]
    if paired:
        partner = [(c, c ^ 1) for c in range(col_count)]
        other = lax.ppermute(bc_pre, "col", partner)
        bc_pre = jnp.where(
            col_index % 2 == 0,
            jnp.concatenate([bc_pre, other], axis=1),
            jnp.concatenate([other, bc_pre], axis=1),
        )
    dt_raw = (
        summed_wide[tok_rows:].reshape(-1)[: heads_dev * tok_rows]
        .reshape(heads_dev, tok_rows)
        .T
    )
    x_pre = xz_sum[:, :, :head_width]
    gate_z = xz_sum[:, :, head_width:]
    edge_len = conv_x.shape[0] - 1
    edge = jnp.concatenate(
        [x_pre[tok_rows - edge_len :].reshape(edge_len, -1), bc_pre[tok_rows - edge_len :]], axis=1
    )
    edge = shifted(edge, "ctx", 1)
    x_edge = edge[:, : heads_dev * head_width].reshape(edge_len, heads_dev, head_width)
    bc_edge = edge[:, heads_dev * head_width :]
    x_conv = causal_conv(x_edge, x_pre, conv_x, conv_x_bias)
    bc_kernel = lax.dynamic_index_in_dim(conv_bc, own_group, 1, keepdims=False)
    bc_offset = lax.dynamic_index_in_dim(conv_bc_bias, own_group, 0, keepdims=False)
    bc_conv = causal_conv(bc_edge, bc_pre, bc_kernel, bc_offset)
    b_input = bc_conv[:, :state_width]
    c_output = bc_conv[:, state_width:]
    step_size = jax.nn.softplus(dt_raw + dt_bias)
    cumul = jnp.cumsum(step_size * jnp.exp(a_log), axis=0)
    cum_heads = cumul.T
    diff = cum_heads[:, :, None] - cum_heads[:, None, :]
    positions = jnp.arange(tok_rows)
    causal = (positions[:, None] >= positions[None, :])[None]
    decay = jnp.where(causal, jnp.exp(-jnp.where(causal, diff, 0.0)), 0.0)
    scores = jnp.einsum("tn,sn->ts", c_output, b_input, preferred_element_type=jnp.float32)
    mixing = (scores[None] * decay * step_size.T[:, None, :]).astype(jnp.bfloat16)
    y_intra = jnp.einsum("hts,shp->thp", mixing, x_conv, preferred_element_type=jnp.float32)
    tail = jnp.exp(-(cumul[-1][None, :] - cumul))
    scaled = ((tail * step_size)[:, :, None] * x_conv.astype(jnp.float32)).astype(jnp.bfloat16)
    local = jnp.einsum("shp,sn->hpn", scaled, b_input, preferred_element_type=jnp.float32)
    fall = jnp.exp(-cumul[-1])
    _, state_in = entering(fall, local, "ctx")
    carried = jnp.einsum(
        "tn,hpn->thp", c_output.astype(jnp.float32), state_in, precision=lax.Precision.HIGHEST
    )
    y_total = (
        y_intra
        + jnp.exp(-cumul)[:, :, None] * carried
        + d_skip[None, :, None] * x_conv.astype(jnp.float32)
    )
    gated = y_total * jax.nn.silu(gate_z.astype(jnp.float32))
    squares = jnp.sum(gated * gated, axis=(1, 2))
    if group_heads == 2 * heads_dev:
        partner = [(c, c ^ 1) for c in range(col_count)]
        group_sum = squares + lax.ppermute(squares, "col", partner)
    else:
        selector = (jnp.arange(groups, dtype=jnp.int32) == own_group).astype(jnp.float32)
        group_sums = lax.psum(squares[:, None] * selector[None, :], ("row", "col"))
        group_sum = jnp.sum(group_sums * selector[None, :], axis=1)
    mean_sq = group_sum / (group_heads * head_width)
    normed = (gated * lax.rsqrt(mean_sq + EPSILON)[:, None, None] * norm_gain).astype(jnp.bfloat16)
    partial_out = jnp.einsum("lhp,hpd->ld", normed, w_out, preferred_element_type=jnp.float32)
    swapped = lax.all_to_all(
        partial_out.astype(jnp.bfloat16), "row", split_axis=1, concat_axis=0, tiled=True
    )
    by_row = jnp.sum(
        swapped.reshape(row_count, tok_rows, -1).astype(jnp.float32), axis=0
    ).astype(jnp.bfloat16)
    crossed = lax.all_to_all(by_row, "col", split_axis=1, concat_axis=0, tiled=True)
    return jnp.sum(crossed.reshape(col_count, tok_rows, -1).astype(jnp.float32), axis=0)


def solution(mesh):
    in_specs = (
        P("ctx", "col"),
        P("col", "row", None),
        P("col", "row"),
        P("col", "row", None),
        P(None, ("row", "col"), None),
        P(("row", "col"), None),
        P(),
        P(),
        P(("row", "col")),
        P(("row", "col")),
        P(("row", "col")),
        P(("row", "col"), None),
        P(("row", "col"), None, None),
    )
    out_specs = P("ctx", ("row", "col"))
    return jax.shard_map(body, mesh=mesh, in_specs=in_specs, out_specs=out_specs, check_vma=False)
```

```python
import jax
import jax.numpy as jnp
from jax import lax
from jax.sharding import PartitionSpec as P

EPSILON = 1e-05


def shifted(block, axis, distance):
    devices = range(lax.axis_size(axis))
    route = [(i - distance, i) for i in devices if i - distance in devices]
    return lax.ppermute(block, axis, route)


def shifted_narrow(block, axis, distance):
    return shifted(block.astype(jnp.bfloat16), axis, distance).astype(block.dtype)


def causal_conv(edge_rows, own_rows, weights, bias):
    width_k = weights.shape[0]
    count = own_rows.shape[0]
    joined = jnp.concatenate([edge_rows, own_rows], axis=0).astype(jnp.float32)
    total = bias + jnp.zeros(own_rows.shape, jnp.float32)
    for offset in range(width_k):
        total = total + weights[offset] * joined[offset : offset + count]
    return jax.nn.silu(total).astype(jnp.bfloat16)


def combine_states(earlier, later):
    return (earlier[0] * later[0], later[0][:, None, None] * earlier[1] + later[1])


def entering(fall, local, axis, radix=4):
    size, mine = lax.axis_size(axis), lax.axis_index(axis)
    rows = local.shape[1]
    own = jnp.concatenate(
        [local, jnp.broadcast_to(fall[:, None, None], (local.shape[0], 1, local.shape[2]))], axis=1
    )
    identity = jnp.concatenate(
        [jnp.zeros_like(local), jnp.ones((local.shape[0], 1, local.shape[2]), local.dtype)], axis=1
    )

    def join(before, later):
        later_fall = later[:, rows : rows + 1, :]
        return jnp.concatenate(
            [later_fall * before[:, :rows] + later[:, :rows], later_fall * before[:, rows:]], axis=1
        )

    acc = identity
    for distance in range(radix, 0, -1):
        if distance < size:
            got = shifted_narrow(own, axis, distance)
            acc = jnp.where(mine >= distance, join(acc, got), acc)
    span = radix
    while span < size:
        parts = [(step * span, shifted_narrow(acc, axis, step * span)) for step in range(1, radix) if step * span < size]
        total = acc
        for distance, got in parts:
            total = jnp.where(mine >= distance, join(got, total), total)
        acc = total
        span *= radix
    return acc[:, rows, 0], acc[:, :rows]


def body(
    tokens,
    w_xz,
    w_dt,
    w_bc,
    conv_x,
    conv_x_bias,
    conv_bc,
    conv_bc_bias,
    dt_bias,
    a_log,
    d_skip,
    norm_gain,
    w_out,
):
    tok_rows = tokens.shape[0]
    row_count = lax.axis_size("row")
    col_count = lax.axis_size("col")
    heads_row = w_xz.shape[1]
    heads_dev = heads_row // col_count
    head_width = w_xz.shape[2] // 2
    groups_row = w_bc.shape[1]
    groups = groups_row * row_count
    state_width = w_bc.shape[2] // 2
    group_heads = heads_row * row_count // groups
    col_index = lax.axis_index("col")
    row_first = lax.axis_index("row") * col_count * heads_dev
    group_start = row_first // group_heads
    own_group = (row_first + col_index * heads_dev) // group_heads
    xz_term = jnp.einsum(
        "hdk,ld->lhk", jnp.transpose(w_xz, (1, 0, 2)), tokens, preferred_element_type=jnp.float32
    )
    dt_term = jnp.dot(tokens, w_dt, preferred_element_type=jnp.float32)
    bc_part = jnp.einsum("ld,dgn->lgn", tokens, w_bc, preferred_element_type=jnp.float32)
    slot_group = (
        row_first + jnp.arange(col_count, dtype=jnp.int32) * heads_dev
    ) // group_heads - group_start
    paired = group_heads == 2 * heads_dev and col_count == 2 * groups_row
    if paired:
        bc_slots = bc_part.reshape(tok_rows, col_count, state_width)
    else:
        bc_slots = jnp.zeros((tok_rows, col_count, 2 * state_width), jnp.float32)
        for member in range(groups_row):
            picked = (slot_group == member).astype(jnp.float32)
            bc_slots = bc_slots + bc_part[:, member][:, None, :] * picked[None, :, None]
    xz_slots = xz_term.reshape(tok_rows, col_count, heads_dev * 2 * head_width)
    main = jnp.concatenate([xz_slots, bc_slots], axis=2)
    feat = main.shape[2]
    dt_flat = dt_term.reshape(tok_rows, col_count, heads_dev).transpose(1, 2, 0).reshape(col_count, -1)
    dt_rows = -(-dt_flat.shape[1] // (8 * feat)) * 8
    dt_flat = jnp.pad(dt_flat, ((0, 0), (0, dt_rows * feat - dt_flat.shape[1])))
    dt_block = dt_flat.reshape(col_count, dt_rows, feat).transpose(1, 0, 2)
    packed = jnp.concatenate([main, dt_block], axis=0)
    summed = lax.optimization_barrier(
        lax.psum_scatter(packed.astype(jnp.bfloat16), "col", scatter_dimension=1, tiled=True)
    )[:, 0]
    xz_width = heads_dev * 2 * head_width
    xz_sum = summed[:tok_rows, :xz_width].reshape(tok_rows, heads_dev, 2 * head_width)
    bc_pre = summed[:tok_rows, xz_width:]
    if paired:
        partner = [(c, c ^ 1) for c in range(col_count)]
        other = lax.ppermute(bc_pre, "col", partner)
        bc_pre = jnp.where(
            col_index % 2 == 0,
            jnp.concatenate([bc_pre, other], axis=1),
            jnp.concatenate([other, bc_pre], axis=1),
        )
    dt_raw = (
        summed[tok_rows:].reshape(-1)[: heads_dev * tok_rows]
        .reshape(heads_dev, tok_rows)
        .T.astype(jnp.float32)
    )
    x_pre = xz_sum[:, :, :head_width]
    gate_z = xz_sum[:, :, head_width:]
    edge_len = conv_x.shape[0] - 1
    edge = jnp.concatenate(
        [x_pre[tok_rows - edge_len :].reshape(edge_len, -1), bc_pre[tok_rows - edge_len :]], axis=1
    )
    edge = shifted(edge, "ctx", 1)
    x_edge = edge[:, : heads_dev * head_width].reshape(edge_len, heads_dev, head_width)
    bc_edge = edge[:, heads_dev * head_width :]
    x_conv = causal_conv(x_edge, x_pre, conv_x, conv_x_bias)
    bc_kernel = lax.dynamic_index_in_dim(conv_bc, own_group, 1, keepdims=False)
    bc_offset = lax.dynamic_index_in_dim(conv_bc_bias, own_group, 0, keepdims=False)
    bc_conv = causal_conv(bc_edge, bc_pre, bc_kernel, bc_offset)
    b_input = bc_conv[:, :state_width]
    c_output = bc_conv[:, state_width:]
    step_size = jax.nn.softplus(dt_raw + dt_bias)
    cumul = jnp.cumsum(step_size * jnp.exp(a_log), axis=0)
    cum_heads = cumul.T
    diff = cum_heads[:, :, None] - cum_heads[:, None, :]
    positions = jnp.arange(tok_rows)
    causal = (positions[:, None] >= positions[None, :])[None]
    decay = jnp.where(causal, jnp.exp(-jnp.where(causal, diff, 0.0)), 0.0)
    scores = jnp.einsum("tn,sn->ts", c_output, b_input, preferred_element_type=jnp.float32)
    mixing = (scores[None] * decay * step_size.T[:, None, :]).astype(jnp.bfloat16)
    y_intra = jnp.einsum("hts,shp->thp", mixing, x_conv, preferred_element_type=jnp.float32)
    tail = jnp.exp(-(cumul[-1][None, :] - cumul))
    scaled = ((tail * step_size)[:, :, None] * x_conv.astype(jnp.float32)).astype(jnp.bfloat16)
    local = jnp.einsum("shp,sn->hpn", scaled, b_input, preferred_element_type=jnp.float32)
    fall = jnp.exp(-cumul[-1])
    _, state_in = entering(fall, local, "ctx")
    carried = jnp.einsum(
        "tn,hpn->thp", c_output.astype(jnp.float32), state_in, precision=lax.Precision.HIGHEST
    )
    y_total = (
        y_intra
        + jnp.exp(-cumul)[:, :, None] * carried
        + d_skip[None, :, None] * x_conv.astype(jnp.float32)
    )
    gated = y_total * jax.nn.silu(gate_z.astype(jnp.float32))
    squares = jnp.sum(gated * gated, axis=(1, 2))
    if group_heads == 2 * heads_dev:
        partner = [(c, c ^ 1) for c in range(col_count)]
        group_sum = squares + lax.ppermute(squares, "col", partner)
    else:
        selector = (jnp.arange(groups, dtype=jnp.int32) == own_group).astype(jnp.float32)
        group_sums = lax.psum(squares[:, None] * selector[None, :], ("row", "col"))
        group_sum = jnp.sum(group_sums * selector[None, :], axis=1)
    mean_sq = group_sum / (group_heads * head_width)
    normed = (gated * lax.rsqrt(mean_sq + EPSILON)[:, None, None] * norm_gain).astype(jnp.bfloat16)
    partial_out = jnp.einsum("lhp,hpd->ld", normed, w_out, preferred_element_type=jnp.float32)
    swapped = lax.all_to_all(
        partial_out.astype(jnp.bfloat16), "row", split_axis=1, concat_axis=0, tiled=True
    )
    by_row = jnp.sum(
        swapped.reshape(row_count, tok_rows, -1).astype(jnp.float32), axis=0
    ).astype(jnp.bfloat16)
    crossed = lax.all_to_all(by_row, "col", split_axis=1, concat_axis=0, tiled=True)
    return jnp.sum(crossed.reshape(col_count, tok_rows, -1).astype(jnp.float32), axis=0)


def solution(mesh):
    in_specs = (
        P("ctx", "col"),
        P("col", "row", None),
        P("col", "row"),
        P("col", "row", None),
        P(None, ("row", "col"), None),
        P(("row", "col"), None),
        P(),
        P(),
        P(("row", "col")),
        P(("row", "col")),
        P(("row", "col")),
        P(("row", "col"), None),
        P(("row", "col"), None, None),
    )
    out_specs = P("ctx", ("row", "col"))
    return jax.shard_map(body, mesh=mesh, in_specs=in_specs, out_specs=out_specs, check_vma=False)
```

```python
import jax
import jax.numpy as jnp
from jax import lax
from jax.sharding import PartitionSpec as P

EPSILON = 1e-05


def shifted(block, axis, distance):
    devices = range(lax.axis_size(axis))
    route = [(i - distance, i) for i in devices if i - distance in devices]
    return lax.ppermute(block, axis, route)


def shifted_narrow(block, axis, distance):
    return shifted(block.astype(jnp.bfloat16), axis, distance).astype(block.dtype)


def causal_conv(edge_rows, own_rows, weights, bias):
    width_k = weights.shape[0]
    count = own_rows.shape[0]
    joined = jnp.concatenate([edge_rows, own_rows], axis=0).astype(jnp.float32)
    total = bias + jnp.zeros(own_rows.shape, jnp.float32)
    for offset in range(width_k):
        total = total + weights[offset] * joined[offset : offset + count]
    return jax.nn.silu(total).astype(jnp.bfloat16)


def combine_states(earlier, later):
    return (earlier[0] * later[0], later[0][:, None, None] * earlier[1] + later[1])


def entering(fall, local, axis, radix=4):
    size, mine = lax.axis_size(axis), lax.axis_index(axis)
    rows = local.shape[1]
    own = jnp.concatenate(
        [local, jnp.broadcast_to(fall[:, None, None], (local.shape[0], 1, local.shape[2]))], axis=1
    )
    identity = jnp.concatenate(
        [jnp.zeros_like(local), jnp.ones((local.shape[0], 1, local.shape[2]), local.dtype)], axis=1
    )

    def join(before, later):
        later_fall = later[:, rows : rows + 1, :]
        return jnp.concatenate(
            [later_fall * before[:, :rows] + later[:, :rows], later_fall * before[:, rows:]], axis=1
        )

    acc = identity
    for distance in range(radix, 0, -1):
        if distance < size:
            got = shifted_narrow(own, axis, distance)
            acc = jnp.where(mine >= distance, join(acc, got), acc)
    span = radix
    while span < size:
        parts = [(step * span, shifted_narrow(acc, axis, step * span)) for step in range(1, radix) if step * span < size]
        total = acc
        for distance, got in parts:
            total = jnp.where(mine >= distance, join(got, total), total)
        acc = total
        span *= radix
    return acc[:, rows, 0], acc[:, :rows]


def body(
    tokens,
    w_xz,
    w_dt,
    w_bc,
    conv_x,
    conv_x_bias,
    conv_bc,
    conv_bc_bias,
    dt_bias,
    a_log,
    d_skip,
    norm_gain,
    w_out,
):
    tok_rows = tokens.shape[0]
    row_count = lax.axis_size("row")
    col_count = lax.axis_size("col")
    heads_row = w_xz.shape[1]
    heads_dev = heads_row // col_count
    head_width = w_xz.shape[2] // 2
    groups_row = w_bc.shape[1]
    groups = groups_row * row_count
    state_width = w_bc.shape[2] // 2
    group_heads = heads_row * row_count // groups
    col_index = lax.axis_index("col")
    row_first = lax.axis_index("row") * col_count * heads_dev
    group_start = row_first // group_heads
    own_group = (row_first + col_index * heads_dev) // group_heads
    xz_term = jnp.dot(
        tokens, w_xz.reshape(w_xz.shape[0], -1), preferred_element_type=jnp.float32
    ).reshape(tok_rows, heads_row, w_xz.shape[2])
    dt_term = jnp.dot(tokens, w_dt, preferred_element_type=jnp.float32)
    bc_part = jnp.einsum("ld,dgn->lgn", tokens, w_bc, preferred_element_type=jnp.float32)
    slot_group = (
        row_first + jnp.arange(col_count, dtype=jnp.int32) * heads_dev
    ) // group_heads - group_start
    paired = group_heads == 2 * heads_dev and col_count == 2 * groups_row
    if paired:
        bc_slots = bc_part.reshape(tok_rows, col_count, state_width)
    else:
        bc_slots = jnp.zeros((tok_rows, col_count, 2 * state_width), jnp.float32)
        for member in range(groups_row):
            picked = (slot_group == member).astype(jnp.float32)
            bc_slots = bc_slots + bc_part[:, member][:, None, :] * picked[None, :, None]
    xz_slots = xz_term.reshape(tok_rows, col_count, heads_dev * 2 * head_width)
    main = jnp.concatenate([xz_slots, bc_slots], axis=2)
    feat = main.shape[2]
    dt_flat = dt_term.reshape(tok_rows, col_count, heads_dev).transpose(1, 2, 0).reshape(col_count, -1)
    dt_rows = -(-dt_flat.shape[1] // feat)
    dt_flat = jnp.pad(dt_flat, ((0, 0), (0, dt_rows * feat - dt_flat.shape[1])))
    dt_block = dt_flat.reshape(col_count, dt_rows, feat).transpose(1, 0, 2)
    packed = jnp.concatenate([main, dt_block], axis=0)
    summed = lax.optimization_barrier(
        lax.psum_scatter(packed.astype(jnp.bfloat16), "col", scatter_dimension=1, tiled=True)
    )[:, 0]
    xz_width = heads_dev * 2 * head_width
    xz_sum = summed[:tok_rows, :xz_width].reshape(tok_rows, heads_dev, 2 * head_width)
    bc_pre = summed[:tok_rows, xz_width:]
    if paired:
        partner = [(c, c ^ 1) for c in range(col_count)]
        other = lax.ppermute(bc_pre, "col", partner)
        bc_pre = jnp.where(
            col_index % 2 == 0,
            jnp.concatenate([bc_pre, other], axis=1),
            jnp.concatenate([other, bc_pre], axis=1),
        )
    dt_raw = (
        summed[tok_rows:].reshape(-1)[: heads_dev * tok_rows]
        .reshape(heads_dev, tok_rows)
        .T.astype(jnp.float32)
    )
    x_pre = xz_sum[:, :, :head_width]
    gate_z = xz_sum[:, :, head_width:]
    edge_len = conv_x.shape[0] - 1
    edge = jnp.concatenate(
        [x_pre[tok_rows - edge_len :].reshape(edge_len, -1), bc_pre[tok_rows - edge_len :]], axis=1
    )
    edge = shifted(edge, "ctx", 1)
    x_edge = edge[:, : heads_dev * head_width].reshape(edge_len, heads_dev, head_width)
    bc_edge = edge[:, heads_dev * head_width :]
    x_conv = causal_conv(x_edge, x_pre, conv_x, conv_x_bias)
    bc_kernel = lax.dynamic_index_in_dim(conv_bc, own_group, 1, keepdims=False)
    bc_offset = lax.dynamic_index_in_dim(conv_bc_bias, own_group, 0, keepdims=False)
    bc_conv = causal_conv(bc_edge, bc_pre, bc_kernel, bc_offset)
    b_input = bc_conv[:, :state_width]
    c_output = bc_conv[:, state_width:]
    step_size = jax.nn.softplus(dt_raw + dt_bias)
    cumul = jnp.cumsum(step_size * jnp.exp(a_log), axis=0)
    cum_heads = cumul.T
    diff = cum_heads[:, :, None] - cum_heads[:, None, :]
    positions = jnp.arange(tok_rows)
    causal = (positions[:, None] >= positions[None, :])[None]
    decay = jnp.where(causal, jnp.exp(-jnp.where(causal, diff, 0.0)), 0.0)
    scores = jnp.einsum("tn,sn->ts", c_output, b_input, preferred_element_type=jnp.float32)
    mixing = (scores[None] * decay * step_size.T[:, None, :]).astype(jnp.bfloat16)
    y_intra = jnp.einsum("hts,shp->thp", mixing, x_conv, preferred_element_type=jnp.float32)
    tail = jnp.exp(-(cumul[-1][None, :] - cumul))
    scaled = ((tail * step_size)[:, :, None] * x_conv.astype(jnp.float32)).astype(jnp.bfloat16)
    local = jnp.einsum("shp,sn->hpn", scaled, b_input, preferred_element_type=jnp.float32)
    fall = jnp.exp(-cumul[-1])
    _, state_in = entering(fall, local, "ctx")
    carried = jnp.einsum(
        "tn,hpn->thp", c_output.astype(jnp.float32), state_in, precision=lax.Precision.HIGHEST
    )
    y_total = (
        y_intra
        + jnp.exp(-cumul)[:, :, None] * carried
        + d_skip[None, :, None] * x_conv.astype(jnp.float32)
    )
    gated = y_total * jax.nn.silu(gate_z.astype(jnp.float32))
    squares = jnp.sum(gated * gated, axis=(1, 2))
    if group_heads == 2 * heads_dev:
        partner = [(c, c ^ 1) for c in range(col_count)]
        group_sum = squares + lax.ppermute(squares, "col", partner)
    else:
        selector = (jnp.arange(groups, dtype=jnp.int32) == own_group).astype(jnp.float32)
        group_sums = lax.psum(squares[:, None] * selector[None, :], ("row", "col"))
        group_sum = jnp.sum(group_sums * selector[None, :], axis=1)
    mean_sq = group_sum / (group_heads * head_width)
    normed = (gated * lax.rsqrt(mean_sq + EPSILON)[:, None, None] * norm_gain).astype(jnp.bfloat16)
    partial_out = jnp.einsum("lhp,hpd->ld", normed, w_out, preferred_element_type=jnp.float32)
    swapped = lax.all_to_all(
        partial_out.astype(jnp.bfloat16), "row", split_axis=1, concat_axis=0, tiled=True
    )
    by_row = jnp.sum(
        swapped.reshape(row_count, tok_rows, -1).astype(jnp.float32), axis=0
    ).astype(jnp.bfloat16)
    crossed = lax.all_to_all(by_row, "col", split_axis=1, concat_axis=0, tiled=True)
    return jnp.sum(crossed.reshape(col_count, tok_rows, -1).astype(jnp.float32), axis=0)


def solution(mesh):
    in_specs = (
        P("ctx", "col"),
        P("col", "row", None),
        P("col", "row"),
        P("col", "row", None),
        P(None, ("row", "col"), None),
        P(("row", "col"), None),
        P(),
        P(),
        P(("row", "col")),
        P(("row", "col")),
        P(("row", "col")),
        P(("row", "col"), None),
        P(("row", "col"), None, None),
    )
    out_specs = P("ctx", ("row", "col"))
    return jax.shard_map(body, mesh=mesh, in_specs=in_specs, out_specs=out_specs, check_vma=False)
```
